32 devices in a mesh: gx: 4 (over z), gy: 2 (over y), gz: 4 (over x, core).
Axes of the slice: x: 2, y: 2, z: 4, core: 2. Of those that a mesh axis runs over, the one named last changes fastest.
Arguments:
- positions: float32 [3, 4, 2, 8, 128], P(None, 'gx', 'gy', 'gz'), may hold values from 0 to 8, as said below
- velocity: float32 [3, 4, 2, 8, 128], P(None, 'gx', 'gy', 'gz'), may hold values from -16 to 16
- counts: int32 [4, 2, 8], P('gx', 'gy', 'gz'), may hold values from 0 to 128, as said below
Outputs:
- velocity_new: float32 [3, 4, 2, 8, 128], P(None, 'gx', 'gy', 'gz')
- pressure: float32 [4, 2, 8, 128], P('gx', 'gy', 'gz')
The draws below stay inside these ranges and needn't reach their ends.
Inputs may be any that keep to these rules, and one draw needn't show every extreme that they name: `positions`: component k of the position of any slot of tile (a, b, c) lies in [t, t + 1), where t is a, b or c for k = 0, 1, 2. A tile's particles fill its first counts[a, b, c] slots. In every column of tiles the bottom tile is full, the tiles below one topmost wet tile hold 96 or more particles, and the tiles above it are empty.
All inputs are finite; a program needn't handle non-finite values.
Results may differ from the reference program's by a relative error of at most 0.0003.
Values sent between devices are 32-bit elements; how exact they have to be, the bound alone decides.
No kernel may reach another device: no remote copies, remote signals or barrier semaphores. Data moves between devices by JAX's collectives and lax.ppermute only.
A program may use at most 64 MiB of HBM per device.

```python
import math
import jax
import jax.numpy as jnp
from jax import lax

P_SIZE = 128
ITERS = 3
NTX = 4
NTY = 2
NTZ = 8


def draw_positions(key, part):
    unit = jax.random.uniform(key, (3, NTX, NTY, NTZ, P_SIZE), jnp.float32, 0.0, 1.0)
    unit = jnp.minimum(unit, 0.999)
    along_x = jnp.broadcast_to(jnp.arange(NTX, dtype=jnp.float32)[:, None, None], (NTX, NTY, NTZ))
    along_y = jnp.broadcast_to(jnp.arange(NTY, dtype=jnp.float32)[None, :, None], (NTX, NTY, NTZ))
    along_z = jnp.broadcast_to(jnp.arange(NTZ, dtype=jnp.float32)[None, None, :], (NTX, NTY, NTZ))
    corner = jnp.stack([along_x, along_y, along_z])[:, :, :, :, None]
    return (corner + unit).astype(jnp.float32)


def draw_velocity(key, part):
    first_key, second_key = jax.random.split(key, 2)
    ramp = 1.0 + 2.0 * jnp.arange(NTY, dtype=jnp.float32) / NTY
    spread = jax.random.uniform(second_key, (1, NTX, NTY, NTZ, 1), jnp.float32, math.log(0.4), math.log(2.5))
    tile_scale = jnp.exp(spread) * ramp[None, None, :, None, None] / 2.0
    base = jnp.clip(jax.random.normal(first_key, (3, NTX, NTY, NTZ, P_SIZE), jnp.float32), -4.0, 4.0)
    return (base * tile_scale).astype(jnp.float32)


def draw_counts(key, part):
    first_key, second_key = jax.random.split(jax.random.fold_in(key, 17), 2)
    along_x = jnp.arange(NTX, dtype=jnp.int32)[:, None, None]
    along_z = jnp.arange(NTZ, dtype=jnp.int32)[None, None, :]
    surface = NTZ * (9 * NTX - 5 * along_x) // (10 * NTX)
    full_tiles = jnp.minimum(jax.random.randint(first_key, (NTX, NTY, NTZ), P_SIZE - P_SIZE // 4, P_SIZE + P_SIZE // 2), P_SIZE)
    top_tiles = jax.random.randint(second_key, (NTX, NTY, NTZ), 1, P_SIZE + 1)
    filled = jnp.where(along_z < surface, full_tiles, jnp.where(along_z == surface, top_tiles, 0))
    filled = jnp.where(along_z == 0, P_SIZE, filled)
    return filled.astype(jnp.int32)


def setup_inputs(seed: int = 0) -> dict:
    key_list = jax.random.split(jax.random.key(seed), 4)
    positions = draw_positions(jax.random.fold_in(key_list[3], 71), 0)
    velocity = draw_velocity(jax.random.fold_in(key_list[3], 71), 0)
    counts = draw_counts(jax.random.fold_in(key_list[3], 71), 0)
    return {"positions": positions, "velocity": velocity, "counts": counts}


DIAG_SHIFT = 0.05
VISCOSITY = 0.5
GRAVITY = 0.1
GRADIENT_GAIN = 32.0


def tile_pairs(rim_positions, rim_valid, rim_field, fold_step, totals):
    size_x = rim_positions.shape[1] - 2
    size_y = rim_positions.shape[2] - 2
    size_z = rim_positions.shape[3] - 2
    slab_tiles = size_y * size_z
    tile_width = rim_positions.shape[4]

    def near_block(source_array, x_start, y_start, z_start):
        zero_start = jnp.zeros((), jnp.int32)
        window = lax.dynamic_slice(source_array, (zero_start, x_start, y_start, z_start, zero_start), (source_array.shape[0], 1, size_y, size_z, tile_width))
        return window.reshape(source_array.shape[0], slab_tiles, tile_width)

    def slab_totals(x_index):
        unit_step = jnp.ones((), jnp.int32)
        own_positions = near_block(rim_positions, x_index + unit_step, unit_step, unit_step)
        own_valid = near_block(rim_valid, x_index + unit_step, unit_step, unit_step)[0]
        start_totals = jax.tree.map(lambda item: jnp.zeros((item.shape[0], slab_tiles, item.shape[2]), jnp.float32), totals)

        def one_offset(offset_index, carry):
            offset_code = jnp.asarray(offset_index).astype(jnp.int32)
            step_x = offset_code // 9
            step_y = (offset_code // 3) % 3
            step_z = offset_code % 3
            near_positions = near_block(rim_positions, x_index + step_x, step_y, step_z)
            near_valid = near_block(rim_valid, x_index + step_x, step_y, step_z)[0]
            near_field = near_block(rim_field, x_index + step_x, step_y, step_z)
            offset = own_positions[:, :, :, None] - near_positions[:, :, None, :]
            distance = offset[0] * offset[0] + offset[1] * offset[1] + offset[2] * offset[2]
            closeness = jnp.maximum(1.0 - distance, 0.0)
            weight = closeness * closeness * own_valid[:, :, None] * near_valid[:, None, :]
            return fold_step(carry, weight, offset, near_field)

        return lax.fori_loop(0, 27, one_offset, start_totals)

    stacked = lax.map(slab_totals, jnp.arange(size_x, dtype=jnp.int32))
    return jax.tree.map(lambda block_out: jnp.moveaxis(block_out, 0, 1).reshape(block_out.shape[1], size_x * slab_tiles, block_out.shape[3]), stacked)


def flat_zeros(rim_positions, components):
    tile_count = (rim_positions.shape[1] - 2) * (rim_positions.shape[2] - 2) * (rim_positions.shape[3] - 2)
    return jnp.zeros((components, tile_count, rim_positions.shape[4]), jnp.float32)


def unflat(flat_values, rim_positions):
    return flat_values.reshape(flat_values.shape[0], rim_positions.shape[1] - 2, rim_positions.shape[2] - 2, rim_positions.shape[3] - 2, flat_values.shape[2])


def viscous_fold(totals, weight, offset, near_field):
    near_sums, row_sums = totals
    near_sums = near_sums + jnp.einsum("tij,ctj->cti", weight, near_field, precision=lax.Precision.HIGHEST)
    return (near_sums, row_sums + jnp.sum(weight, axis=2)[None])


def divergence_fold(totals, weight, offset, near_field):
    lever_sums, flux_sums = totals
    levered = weight[None] * offset
    flux_sums = flux_sums + jnp.einsum("ctij,ctj->ti", levered, near_field, precision=lax.Precision.HIGHEST)[None]
    return (lever_sums + jnp.sum(levered, axis=3), flux_sums)


def laplace_fold(totals, weight, offset, near_field):
    return totals + jnp.einsum("tij,ctj->cti", weight, near_field, precision=lax.Precision.HIGHEST)


def gradient_fold(totals, weight, offset, near_field):
    levered = weight[None] * offset
    return totals + jnp.einsum("ctij,tj->cti", levered, near_field[0], precision=lax.Precision.HIGHEST)


def viscous_pass(rim_positions, rim_valid, rim_field):
    near_sums, row_sums = tile_pairs(rim_positions, rim_valid, rim_field, viscous_fold, (flat_zeros(rim_positions, 3), flat_zeros(rim_positions, 1)))
    return unflat(near_sums, rim_positions), unflat(row_sums, rim_positions)


def divergence_pass(rim_positions, rim_valid, rim_field):
    lever_sums, flux_sums = tile_pairs(rim_positions, rim_valid, rim_field, divergence_fold, (flat_zeros(rim_positions, 3), flat_zeros(rim_positions, 1)))
    return unflat(lever_sums, rim_positions), unflat(flux_sums, rim_positions)


def laplace_pass(rim_positions, rim_valid, rim_field):
    return unflat(tile_pairs(rim_positions, rim_valid, rim_field, laplace_fold, flat_zeros(rim_positions, 1)), rim_positions)


def gradient_pass(rim_positions, rim_valid, rim_field):
    return unflat(tile_pairs(rim_positions, rim_valid, rim_field, gradient_fold, flat_zeros(rim_positions, 3)), rim_positions)


def advance(velocity, valid_mask, near_sums, row_sums):
    gravity_pull = jnp.array([0.0, 0.0, -GRAVITY], jnp.float32).reshape(3, 1, 1, 1, 1)
    return valid_mask * (velocity + VISCOSITY / P_SIZE * (near_sums - row_sums * velocity) + gravity_pull)


def padded_grid(field):
    return jnp.pad(field, ((0, 0), (1, 1), (1, 1), (1, 1), (0, 0)))


def sweep_slabs(function, padded):
    def slab_view(slab_index):
        return function(*[lax.dynamic_slice_in_dim(item, slab_index, 3, 1) for item in padded])

    stacked = lax.map(slab_view, jnp.arange(NTX, dtype=jnp.int32))
    return jax.tree.map(lambda block_out: jnp.moveaxis(block_out, 0, 1).reshape((block_out.shape[1], NTX) + block_out.shape[3:]), stacked)


def reference(positions, velocity, counts):
    slot_ids = jnp.arange(P_SIZE, dtype=jnp.int32)
    valid_mask = (slot_ids[None, None, None, :] < counts[:, :, :, None]).astype(jnp.float32)[None]
    pad_positions = padded_grid(positions)
    pad_valid = padded_grid(valid_mask)
    near_sums, row_sums = sweep_slabs(viscous_pass, [pad_positions, pad_valid, padded_grid(velocity)])
    predicted = advance(velocity, valid_mask, near_sums, row_sums)
    diagonal = DIAG_SHIFT + row_sums / P_SIZE
    lever_sums, flux_sums = sweep_slabs(divergence_pass, [pad_positions, pad_valid, padded_grid(predicted)])
    source = -(GRADIENT_GAIN / P_SIZE) * (jnp.sum(predicted * lever_sums, axis=0, keepdims=True) - flux_sums)
    pressure = jnp.zeros_like(source)
    residual = source
    precond = residual / diagonal
    direction = precond
    norm_now = jnp.sum(residual * precond)
    for iteration in range(ITERS):
        applied = diagonal * direction - sweep_slabs(laplace_pass, [pad_positions, pad_valid, padded_grid(direction)]) / P_SIZE
        step_size = norm_now / jnp.sum(direction * applied)
        pressure = pressure + step_size * direction
        residual = residual - step_size * applied
        if iteration + 1 < ITERS:
            precond = residual / diagonal
            norm_next = jnp.sum(residual * precond)
            direction = precond + (norm_next / norm_now) * direction
            norm_now = norm_next
    moments = sweep_slabs(gradient_pass, [pad_positions, pad_valid, padded_grid(pressure)])
    velocity_new = predicted - (GRADIENT_GAIN / P_SIZE) * (pressure * lever_sums - moments)
    return velocity_new, pressure[0]
```

```python
import jax
import jax.numpy as jnp
from jax import lax
from jax.sharding import PartitionSpec as P

ITERS = 3

DIAG_SHIFT = 0.05
VISCOSITY = 0.5
GRAVITY = 0.1
GRADIENT_GAIN = 32.0

AXES = (("gx", 1), ("gy", 2), ("gz", 3))


def with_halo(cells, sides, width):
    for axis, dim in sides:
        count = lax.axis_size(axis)
        ends = count - 1
        head = lax.slice_in_dim(cells, 0, width, axis=dim)
        tail = lax.slice_in_dim(cells, cells.shape[dim] - width, cells.shape[dim], axis=dim)
        cells = jnp.concatenate(
            [
                lax.ppermute(tail, axis, [(i, (i + 1) % count) for i in range(ends)]),
                cells,
                lax.ppermute(head, axis, [((i + 1) % count, i) for i in range(ends)]),
            ],
            axis=dim,
        )
    return cells


def neighbours(rim):
    comps, size_x, size_y, size_z, width = rim.shape
    blocks = []
    for ax in range(size_x - 2):
        for ay in range(size_y - 2):
            for az in range(size_z - 2):
                window = rim[:, ax:ax + 3, ay:ay + 3, az:az + 3, :]
                blocks.append(window.reshape(comps, 27 * width))
    return jnp.stack(blocks, axis=1)


def flat(cells):
    return cells.reshape(cells.shape[0], -1, cells.shape[4])


def wsum(weight, near):
    return jnp.sum(weight[None] * near[:, :, None, :], axis=-1)


def tile_corners(block_shape):
    _, size_x, size_y, size_z, _ = block_shape
    base = (
        lax.axis_index("gx") * size_x,
        lax.axis_index("gy") * size_y,
        lax.axis_index("gz") * size_z,
    )
    corners = []
    for ax in range(size_x):
        for ay in range(size_y):
            for az in range(size_z):
                corners.append(jnp.stack([base[0] + ax, base[1] + ay, base[2] + az]))
    return jnp.stack(corners, axis=1).astype(jnp.float32)


def on_device(positions, velocity, counts):
    block_shape = positions.shape
    width = positions.shape[4]
    slot_ids = jnp.arange(width, dtype=jnp.int32)
    valid_mask = (slot_ids[None, None, None, :] < counts[:, :, :, None]).astype(jnp.float32)[None]
    packed = jnp.concatenate([positions, valid_mask, velocity], axis=0)
    near_all = neighbours(with_halo(packed, AXES, 1))
    near_x = near_all[0:3]
    near_valid = near_all[3]
    near_v = near_all[4:7]
    own_x = flat(positions)
    own_valid = flat(valid_mask)[0]
    own_v = flat(velocity)

    offset = own_x[:, :, :, None] - near_x[:, :, None, :]
    distance = offset[0] * offset[0] + offset[1] * offset[1] + offset[2] * offset[2]
    closeness = jnp.maximum(1.0 - distance, 0.0)
    weight = closeness * closeness * own_valid[:, :, None] * near_valid[:, None, :]

    corner = tile_corners(block_shape)[:, :, None]
    local_own = own_x - corner
    local_near = near_x - corner

    row = jnp.sum(weight, axis=-1)[None]
    sums = wsum(weight, jnp.concatenate([near_v, local_near], axis=0))
    near_sums = sums[0:3]
    lever = local_own * row - sums[3:6]

    gravity_pull = jnp.array([0.0, 0.0, -GRAVITY], jnp.float32).reshape(3, 1, 1)
    predicted = own_valid[None] * (
        own_v + VISCOSITY / width * (near_sums - row * own_v) + gravity_pull
    )
    diagonal = DIAG_SHIFT + row / width

    def shaped(values):
        return values.reshape(values.shape[0], *block_shape[1:])

    near_pred = neighbours(with_halo(shaped(predicted), AXES, 1))
    dotted = jnp.sum(near_pred * local_near, axis=0, keepdims=True)
    psums = wsum(weight, jnp.concatenate([near_pred, dotted], axis=0))
    flux = jnp.sum(local_own * psums[0:3], axis=0, keepdims=True) - psums[3:4]
    source = -(GRADIENT_GAIN / width) * (
        jnp.sum(predicted * lever, axis=0, keepdims=True) - flux
    )

    def operate(field):
        near_field = neighbours(with_halo(shaped(field), AXES, 1))
        return near_field, diagonal * field - wsum(weight, near_field) / width

    def paired_sums(residual, precond, applied):
        pair = jnp.stack([jnp.sum(residual * precond), jnp.sum(precond * applied)])
        total = lax.psum(pair, ("gx", "gy", "gz"))
        return total[0], total[1]

    pressure = jnp.zeros_like(source)
    residual = source
    precond = residual / diagonal
    near_dir, applied = operate(precond)
    norm_now, curvature_sum = paired_sums(residual, precond, applied)
    step_size = norm_now / curvature_sum
    direction = precond
    along = applied
    near_pressure = jnp.zeros_like(near_dir)
    for iteration in range(ITERS):
        pressure = pressure + step_size * direction
        near_pressure = near_pressure + step_size * near_dir
        residual = residual - step_size * along
        if iteration + 1 < ITERS:
            precond = residual / diagonal
            near_fresh, applied = operate(precond)
            norm_next, curvature_sum = paired_sums(residual, precond, applied)
            blend = norm_next / norm_now
            step_size = norm_next / (curvature_sum - blend * norm_next / step_size)
            direction = precond + blend * direction
            near_dir = near_fresh + blend * near_dir
            along = applied + blend * along
            norm_now = norm_next

    grads = wsum(weight, jnp.concatenate([near_pressure, near_pressure * local_near], axis=0))
    moments = local_own * grads[0:1] - grads[1:4]
    velocity_new = predicted - GRADIENT_GAIN / width * (pressure * lever - moments)
    return (shaped(velocity_new), shaped(pressure)[0])


def solution(mesh):
    in_specs = (
        P(None, "gx", "gy", "gz", None),
        P(None, "gx", "gy", "gz", None),
        P("gx", "gy", "gz"),
    )
    out_specs = (P(None, "gx", "gy", "gz", None), P("gx", "gy", "gz", None))
    return jax.shard_map(
        on_device, mesh=mesh, in_specs=in_specs, out_specs=out_specs, check_vma=False
    )
```

```python
import jax
import jax.numpy as jnp
from jax import lax
from jax.sharding import PartitionSpec as P

ITERS = 3

DIAG_SHIFT = 0.05
VISCOSITY = 0.5
GRAVITY = 0.1
GRADIENT_GAIN = 32.0

AXES = (("gx", 1), ("gy", 2), ("gz", 3))


def with_halo(cells, sides, width):
    for axis, dim in sides:
        count = lax.axis_size(axis)
        ends = count - 1
        head = lax.slice_in_dim(cells, 0, width, axis=dim)
        tail = lax.slice_in_dim(cells, cells.shape[dim] - width, cells.shape[dim], axis=dim)
        if count == 2:
            first = lax.axis_index(axis) == 0
            got = lax.ppermute(jnp.where(first, tail, head), axis, [(0, 1), (1, 0)])
            empty = jnp.zeros_like(got)
            cells = jnp.concatenate(
                [jnp.where(first, empty, got), cells, jnp.where(first, got, empty)], axis=dim
            )
            continue
        cells = jnp.concatenate(
            [
                lax.ppermute(tail, axis, [(i, (i + 1) % count) for i in range(ends)]),
                cells,
                lax.ppermute(head, axis, [((i + 1) % count, i) for i in range(ends)]),
            ],
            axis=dim,
        )
    return cells


def total(values):
    for axis in ("gx", "gy", "gz"):
        count = lax.axis_size(axis)
        if count & (count - 1):
            values = lax.psum(values, axis)
            continue
        step = 1
        while step < count:
            values = values + lax.ppermute(values, axis, [(i, i ^ step) for i in range(count)])
            step *= 2
    return values


def neighbours(rim):
    comps, size_x, size_y, size_z, width = rim.shape
    blocks = []
    for ax in range(size_x - 2):
        for ay in range(size_y - 2):
            for az in range(size_z - 2):
                window = rim[:, ax:ax + 3, ay:ay + 3, az:az + 3, :]
                blocks.append(window.reshape(comps, 27 * width))
    return jnp.stack(blocks, axis=1)


def flat(cells):
    return cells.reshape(cells.shape[0], -1, cells.shape[4])


def wsum(weight, near):
    return jnp.sum(weight[None] * near[:, :, None, :], axis=-1)


def tile_corners(block_shape):
    _, size_x, size_y, size_z, _ = block_shape
    base = (
        lax.axis_index("gx") * size_x,
        lax.axis_index("gy") * size_y,
        lax.axis_index("gz") * size_z,
    )
    corners = []
    for ax in range(size_x):
        for ay in range(size_y):
            for az in range(size_z):
                corners.append(jnp.stack([base[0] + ax, base[1] + ay, base[2] + az]))
    return jnp.stack(corners, axis=1).astype(jnp.float32)


def on_device(positions, velocity, counts):
    block_shape = positions.shape
    width = positions.shape[4]
    slot_ids = jnp.arange(width, dtype=jnp.int32)
    valid_mask = (slot_ids[None, None, None, :] < counts[:, :, :, None]).astype(jnp.float32)[None]
    packed = jnp.concatenate([positions, valid_mask, velocity], axis=0)
    near_all = neighbours(with_halo(packed, AXES, 1))
    near_x = near_all[0:3]
    near_valid = near_all[3]
    near_v = near_all[4:7]
    own_x = flat(positions)
    own_valid = flat(valid_mask)[0]
    own_v = flat(velocity)

    offset = own_x[:, :, :, None] - near_x[:, :, None, :]
    distance = offset[0] * offset[0] + offset[1] * offset[1] + offset[2] * offset[2]
    closeness = jnp.maximum(1.0 - distance, 0.0)
    weight = closeness * closeness * own_valid[:, :, None] * near_valid[:, None, :]

    corner = tile_corners(block_shape)[:, :, None]
    local_own = own_x - corner
    local_near = near_x - corner

    row = jnp.sum(weight, axis=-1)[None]
    sums = wsum(weight, jnp.concatenate([near_v, local_near], axis=0))
    near_sums = sums[0:3]
    lever = local_own * row - sums[3:6]

    gravity_pull = jnp.array([0.0, 0.0, -GRAVITY], jnp.float32).reshape(3, 1, 1)
    predicted = own_valid[None] * (
        own_v + VISCOSITY / width * (near_sums - row * own_v) + gravity_pull
    )
    diagonal = DIAG_SHIFT + row / width

    def shaped(values):
        return values.reshape(values.shape[0], *block_shape[1:])

    near_pred = neighbours(with_halo(shaped(predicted), AXES, 1))
    dotted = jnp.sum(near_pred * local_near, axis=0, keepdims=True)
    psums = wsum(weight, jnp.concatenate([near_pred, dotted], axis=0))
    flux = jnp.sum(local_own * psums[0:3], axis=0, keepdims=True) - psums[3:4]
    source = -(GRADIENT_GAIN / width) * (
        jnp.sum(predicted * lever, axis=0, keepdims=True) - flux
    )

    def spread(field):
        near_field = neighbours(with_halo(shaped(field), AXES, 1))
        return near_field, -(wsum(weight, near_field) / width) / diagonal

    basis = [source / diagonal]
    near_basis = []
    for _ in range(ITERS):
        near_field, following = spread(basis[-1])
        near_basis.append(near_field)
        basis.append(following)
    stacked = jnp.concatenate(basis, axis=0)
    weighted = stacked * diagonal
    gram = total(jnp.sum(weighted[:, None] * stacked[None, :], axis=(2, 3)))
    size = ITERS + 1

    def shift_add(coords):
        return coords + jnp.concatenate([jnp.zeros((1,), coords.dtype), coords[:-1]])

    def quad(left, right):
        return jnp.sum(left * jnp.sum(gram * right[None, :], axis=1))

    resid = jnp.zeros((size,), jnp.float32).at[0].set(1.0)
    along = resid
    coords = jnp.zeros((size,), jnp.float32)
    norm_now = quad(resid, resid)
    for iteration in range(ITERS):
        applied = shift_add(along)
        step_size = norm_now / quad(along, applied)
        coords = coords + step_size * along
        resid = resid - step_size * applied
        if iteration + 1 < ITERS:
            norm_next = quad(resid, resid)
            along = resid + (norm_next / norm_now) * along
            norm_now = norm_next
    pressure = jnp.sum(coords[:ITERS, None, None] * stacked[:ITERS], axis=0, keepdims=True)
    near_pressure = coords[0] * near_basis[0]
    for k in range(1, ITERS):
        near_pressure = near_pressure + coords[k] * near_basis[k]

    grads = wsum(weight, jnp.concatenate([near_pressure, near_pressure * local_near], axis=0))
    moments = local_own * grads[0:1] - grads[1:4]
    velocity_new = predicted - GRADIENT_GAIN / width * (pressure * lever - moments)
    return (shaped(velocity_new), shaped(pressure)[0])


def solution(mesh):
    in_specs = (
        P(None, "gx", "gy", "gz", None),
        P(None, "gx", "gy", "gz", None),
        P("gx", "gy", "gz"),
    )
    out_specs = (P(None, "gx", "gy", "gz", None), P("gx", "gy", "gz", None))
    return jax.shard_map(
        on_device, mesh=mesh, in_specs=in_specs, out_specs=out_specs, check_vma=False
    )
```

```python
import jax
import numpy as np
import jax.numpy as jnp
from jax import lax
from jax.sharding import PartitionSpec as P

ITERS = 3

DIAG_SHIFT = 0.05
VISCOSITY = 0.5
GRAVITY = 0.1
GRADIENT_GAIN = 32.0

AXES = (("gx", 1), ("gy", 2), ("gz", 3))


def with_halo(cells, sides, width):
    for axis, dim in sides:
        count = lax.axis_size(axis)
        ends = count - 1
        head = lax.slice_in_dim(cells, 0, width, axis=dim)
        tail = lax.slice_in_dim(cells, cells.shape[dim] - width, cells.shape[dim], axis=dim)
        if count == 2:
            first = lax.axis_index(axis) == 0
            got = lax.ppermute(jnp.where(first, tail, head), axis, [(0, 1), (1, 0)])
            empty = jnp.zeros_like(got)
            cells = jnp.concatenate(
                [jnp.where(first, empty, got), cells, jnp.where(first, got, empty)], axis=dim
            )
            continue
        cells = jnp.concatenate(
            [
                lax.ppermute(tail, axis, [(i, (i + 1) % count) for i in range(ends)]),
                cells,
                lax.ppermute(head, axis, [((i + 1) % count, i) for i in range(ends)]),
            ],
            axis=dim,
        )
    return cells


def total(values):
    for axis in ("gx", "gy", "gz"):
        count = lax.axis_size(axis)
        if count & (count - 1):
            values = lax.psum(values, axis)
            continue
        step = 1
        while step < count:
            values = values + lax.ppermute(values, axis, [(i, i ^ step) for i in range(count)])
            step *= 2
    return values


def neighbours(rim):
    comps, size_x, size_y, size_z, width = rim.shape
    blocks = []
    for ax in range(size_x - 2):
        for ay in range(size_y - 2):
            for az in range(size_z - 2):
                window = rim[:, ax:ax + 3, ay:ay + 3, az:az + 3, :]
                blocks.append(window.reshape(comps, 27 * width))
    return jnp.stack(blocks, axis=1)


def flat(cells):
    return cells.reshape(cells.shape[0], -1, cells.shape[4])


def wsum(weight, near):
    return jnp.sum(weight[None] * near[:, :, None, :], axis=-1)


def tile_corners(block_shape):
    _, size_x, size_y, size_z, _ = block_shape
    base = (
        lax.axis_index("gx") * size_x,
        lax.axis_index("gy") * size_y,
        lax.axis_index("gz") * size_z,
    )
    corners = []
    for ax in range(size_x):
        for ay in range(size_y):
            for az in range(size_z):
                corners.append(jnp.stack([base[0] + ax, base[1] + ay, base[2] + az]))
    return jnp.stack(corners, axis=1).astype(jnp.float32)


def adjacency(block_shape):
    _, size_x, size_y, size_z, width = block_shape
    rows = []
    for ax in range(size_x):
        for ay in range(size_y):
            for az in range(size_z):
                near = np.zeros((size_x + 2, size_y + 2, size_z + 2), np.float32)
                near[ax:ax + 3, ay:ay + 3, az:az + 3] = 1.0
                rows.append(np.repeat(near.reshape(-1), width))
    return np.stack(rows)


def solve3(matrix, rhs):
    h = [[matrix[i, j] for j in range(3)] for i in range(3)]
    g = [rhs[i] for i in range(3)]
    m1 = h[1][0] / h[0][0]
    m2 = h[2][0] / h[0][0]
    a11 = h[1][1] - m1 * h[0][1]
    a12 = h[1][2] - m1 * h[0][2]
    b1 = g[1] - m1 * g[0]
    a21 = h[2][1] - m2 * h[0][1]
    a22 = h[2][2] - m2 * h[0][2]
    b2 = g[2] - m2 * g[0]
    m3 = a21 / a11
    y2 = (b2 - m3 * b1) / (a22 - m3 * a12)
    y1 = (b1 - a12 * y2) / a11
    y0 = (g[0] - h[0][1] * y1 - h[0][2] * y2) / h[0][0]
    return (y0, y1, y2)


def on_device(positions, velocity, counts):
    block_shape = positions.shape
    width = positions.shape[4]
    slot_ids = jnp.arange(width, dtype=jnp.int32)
    valid_mask = (slot_ids[None, None, None, :] < counts[:, :, :, None]).astype(jnp.float32)[None]
    packed = jnp.concatenate([positions, valid_mask, velocity], axis=0)

    def rim_flat(cells):
        rim = with_halo(cells, AXES, 1)
        return rim.reshape(rim.shape[0], 1, -1)

    near_all = rim_flat(packed)
    near_x = near_all[0:3]
    near_valid = near_all[3]
    near_v = near_all[4:7]
    own_x = flat(positions)
    own_valid = flat(valid_mask)[0]
    own_v = flat(velocity)
    tiles = own_x.shape[1]

    offset = own_x[:, :, :, None] - near_x[:, :, None, :]
    distance = offset[0] * offset[0] + offset[1] * offset[1] + offset[2] * offset[2]
    closeness = jnp.maximum(1.0 - distance, 0.0)
    weight = (
        closeness * closeness * own_valid[:, :, None] * near_valid[:, None, :]
    ) * jnp.asarray(adjacency(block_shape))[:, None, :]

    corner = tile_corners(block_shape)[:, :, None]
    local_own = own_x - corner
    local_near = near_x - corner

    def spread_t(near_field):
        return jnp.broadcast_to(near_field, (near_field.shape[0], tiles, near_field.shape[2]))

    row = jnp.sum(weight, axis=-1)[None]
    sums = wsum(weight, jnp.concatenate([spread_t(near_v), local_near], axis=0))
    near_sums = sums[0:3]
    lever = local_own * row - sums[3:6]

    gravity_pull = jnp.array([0.0, 0.0, -GRAVITY], jnp.float32).reshape(3, 1, 1)
    predicted = own_valid[None] * (
        own_v + VISCOSITY / width * (near_sums - row * own_v) + gravity_pull
    )
    diagonal = DIAG_SHIFT + row / width

    def shaped(values):
        return values.reshape(values.shape[0], *block_shape[1:])

    near_pred = rim_flat(shaped(predicted))
    dotted = jnp.sum(near_pred * local_near, axis=0, keepdims=True)
    psums = wsum(weight, jnp.concatenate([spread_t(near_pred), dotted], axis=0))
    flux = jnp.sum(local_own * psums[0:3], axis=0, keepdims=True) - psums[3:4]
    source = -(GRADIENT_GAIN / width) * (
        jnp.sum(predicted * lever, axis=0, keepdims=True) - flux
    )

    basis = [source / diagonal]
    near_w = []
    near_wx = []
    for _ in range(ITERS):
        near_u = rim_flat(shaped(basis[-1]))
        out = wsum(weight, jnp.concatenate([spread_t(near_u), near_u * local_near], axis=0))
        near_w.append(out[0:1])
        near_wx.append(out[1:4])
        basis.append(-(out[0:1] / width) / diagonal)
    stacked = jnp.concatenate(basis, axis=0)
    weighted = stacked[:ITERS] * diagonal
    gram = total(jnp.sum(weighted[:, None] * stacked[None, :], axis=(2, 3)))
    coords = solve3(gram[:, :ITERS] + gram[:, 1:], gram[:, 0])

    pressure = coords[0] * basis[0]
    applied = coords[0] * near_w[0]
    applied_x = coords[0] * near_wx[0]
    for k in range(1, ITERS):
        pressure = pressure + coords[k] * basis[k]
        applied = applied + coords[k] * near_w[k]
        applied_x = applied_x + coords[k] * near_wx[k]
    moments = local_own * applied - applied_x
    velocity_new = predicted - GRADIENT_GAIN / width * (pressure * lever - moments)
    return (shaped(velocity_new), shaped(pressure)[0])


def solution(mesh):
    in_specs = (
        P(None, "gx", "gy", "gz", None),
        P(None, "gx", "gy", "gz", None),
        P("gx", "gy", "gz"),
    )
    out_specs = (P(None, "gx", "gy", "gz", None), P("gx", "gy", "gz", None))
    return jax.shard_map(
        on_device, mesh=mesh, in_specs=in_specs, out_specs=out_specs, check_vma=False
    )
```

```python
import jax
import numpy as np
import jax.numpy as jnp
from jax import lax
from jax.sharding import PartitionSpec as P

ITERS = 3

DIAG_SHIFT = 0.05
VISCOSITY = 0.5
GRAVITY = 0.1
GRADIENT_GAIN = 32.0

AXES = (("gx", 1), ("gy", 2), ("gz", 3))


def with_halo(cells, sides, width):
    for axis, dim in sides:
        count = lax.axis_size(axis)
        ends = count - 1
        head = lax.slice_in_dim(cells, 0, width, axis=dim)
        tail = lax.slice_in_dim(cells, cells.shape[dim] - width, cells.shape[dim], axis=dim)
        if count == 2:
            first = lax.axis_index(axis) == 0
            got = lax.ppermute(jnp.where(first, tail, head), axis, [(0, 1), (1, 0)])
            empty = jnp.zeros_like(got)
            cells = jnp.concatenate(
                [jnp.where(first, empty, got), cells, jnp.where(first, got, empty)], axis=dim
            )
            continue
        cells = jnp.concatenate(
            [
                lax.ppermute(tail, axis, [(i, (i + 1) % count) for i in range(ends)]),
                cells,
                lax.ppermute(head, axis, [((i + 1) % count, i) for i in range(ends)]),
            ],
            axis=dim,
        )
    return cells


def total(values):
    for axis in ("gx", "gy", "gz"):
        count = lax.axis_size(axis)
        if count & (count - 1):
            values = lax.psum(values, axis)
            continue
        step = 1
        while step < count:
            values = values + lax.ppermute(values, axis, [(i, i ^ step) for i in range(count)])
            step *= 2
    return values


def neighbours(rim):
    comps, size_x, size_y, size_z, width = rim.shape
    blocks = []
    for ax in range(size_x - 2):
        for ay in range(size_y - 2):
            for az in range(size_z - 2):
                window = rim[:, ax:ax + 3, ay:ay + 3, az:az + 3, :]
                blocks.append(window.reshape(comps, 27 * width))
    return jnp.stack(blocks, axis=1)


def flat(cells):
    return cells.reshape(cells.shape[0], -1, cells.shape[4])


def wsum(weight, near):
    return jnp.sum(weight[None] * near[:, :, None, :], axis=-1)


def tile_corners(block_shape):
    _, size_x, size_y, size_z, _ = block_shape
    base = (
        lax.axis_index("gx") * size_x,
        lax.axis_index("gy") * size_y,
        lax.axis_index("gz") * size_z,
    )
    corners = []
    for ax in range(size_x):
        for ay in range(size_y):
            for az in range(size_z):
                corners.append(jnp.stack([base[0] + ax, base[1] + ay, base[2] + az]))
    return jnp.stack(corners, axis=1).astype(jnp.float32)


def adjacency(block_shape):
    _, size_x, size_y, size_z, width = block_shape
    rows = []
    for ax in range(size_x):
        for ay in range(size_y):
            for az in range(size_z):
                near = np.zeros((size_x + 2, size_y + 2, size_z + 2), np.float32)
                near[ax:ax + 3, ay:ay + 3, az:az + 3] = 1.0
                rows.append(np.repeat(near.reshape(-1), width))
    return np.stack(rows)


def solve3(matrix, rhs):
    h = [[matrix[i, j] for j in range(3)] for i in range(3)]
    g = [rhs[i] for i in range(3)]
    m1 = h[1][0] / h[0][0]
    m2 = h[2][0] / h[0][0]
    a11 = h[1][1] - m1 * h[0][1]
    a12 = h[1][2] - m1 * h[0][2]
    b1 = g[1] - m1 * g[0]
    a21 = h[2][1] - m2 * h[0][1]
    a22 = h[2][2] - m2 * h[0][2]
    b2 = g[2] - m2 * g[0]
    m3 = a21 / a11
    y2 = (b2 - m3 * b1) / (a22 - m3 * a12)
    y1 = (b1 - a12 * y2) / a11
    y0 = (g[0] - h[0][1] * y1 - h[0][2] * y2) / h[0][0]
    return (y0, y1, y2)


def on_device(positions, velocity, counts):
    block_shape = positions.shape
    width = positions.shape[4]
    slot_ids = jnp.arange(width, dtype=jnp.int32)
    valid_mask = (slot_ids[None, None, None, :] < counts[:, :, :, None]).astype(jnp.float32)[None]
    packed = jnp.concatenate([positions, valid_mask, velocity], axis=0)

    def rim_flat(cells):
        rim = with_halo(cells, AXES, 1)
        return rim.reshape(rim.shape[0], 1, -1)

    near_all = rim_flat(packed)
    near_x = near_all[0:3]
    near_valid = near_all[3]
    near_v = near_all[4:7]
    own_x = flat(positions)
    own_valid = flat(valid_mask)[0]
    own_v = flat(velocity)
    tiles = own_x.shape[1]

    offset = own_x[:, :, :, None] - near_x[:, :, None, :]
    distance = offset[0] * offset[0] + offset[1] * offset[1] + offset[2] * offset[2]
    closeness = jnp.maximum(1.0 - distance, 0.0)
    weight = (
        closeness * closeness * own_valid[:, :, None] * near_valid[:, None, :]
    ) * jnp.asarray(adjacency(block_shape))[:, None, :]

    corner = tile_corners(block_shape)[:, :, None]
    local_own = own_x - corner
    local_near = near_x - corner

    def spread_t(near_field):
        return jnp.broadcast_to(near_field, (near_field.shape[0], tiles, near_field.shape[2]))

    later_weight = lax.optimization_barrier(weight)
    row = jnp.sum(weight, axis=-1)[None]
    near_sums = wsum(weight, spread_t(near_v))
    lever = local_own * row - wsum(later_weight, local_near)

    gravity_pull = jnp.array([0.0, 0.0, -GRAVITY], jnp.float32).reshape(3, 1, 1)
    predicted = own_valid[None] * (
        own_v + VISCOSITY / width * (near_sums - row * own_v) + gravity_pull
    )
    diagonal = DIAG_SHIFT + row / width

    def shaped(values):
        return values.reshape(values.shape[0], *block_shape[1:])

    near_pred = rim_flat(shaped(predicted))
    dotted = jnp.sum(near_pred * local_near, axis=0, keepdims=True)
    psums = wsum(weight, jnp.concatenate([spread_t(near_pred), dotted], axis=0))
    flux = jnp.sum(local_own * psums[0:3], axis=0, keepdims=True) - psums[3:4]
    source = -(GRADIENT_GAIN / width) * (
        jnp.sum(predicted * lever, axis=0, keepdims=True) - flux
    )

    basis = [source / diagonal]
    near_w = []
    near_wx = []
    for _ in range(ITERS):
        near_u = rim_flat(shaped(basis[-1]))
        out = wsum(weight, spread_t(near_u))
        near_w.append(out)
        near_wx.append(wsum(later_weight, near_u * local_near))
        basis.append(-(out / width) / diagonal)
    stacked = jnp.concatenate(basis, axis=0)
    weighted = stacked[:ITERS] * diagonal
    gram = total(jnp.sum(weighted[:, None] * stacked[None, :], axis=2))
    shift = width // 2
    while shift >= 1:
        gram = gram + jnp.roll(gram, shift, axis=-1)
        shift //= 2
    coords = solve3(gram[:, :ITERS] + gram[:, 1:], gram[:, 0])

    pressure = coords[0] * basis[0]
    applied = coords[0] * near_w[0]
    applied_x = coords[0] * near_wx[0]
    for k in range(1, ITERS):
        pressure = pressure + coords[k] * basis[k]
        applied = applied + coords[k] * near_w[k]
        applied_x = applied_x + coords[k] * near_wx[k]
    moments = local_own * applied - applied_x
    velocity_new = predicted - GRADIENT_GAIN / width * (pressure * lever - moments)
    return (shaped(velocity_new), shaped(pressure)[0])


def solution(mesh):
    in_specs = (
        P(None, "gx", "gy", "gz", None),
        P(None, "gx", "gy", "gz", None),
        P("gx", "gy", "gz"),
    )
    out_specs = (P(None, "gx", "gy", "gz", None), P("gx", "gy", "gz", None))
    return jax.shard_map(
        on_device, mesh=mesh, in_specs=in_specs, out_specs=out_specs, check_vma=False
    )
```

```python
import jax
import numpy as np
import jax.numpy as jnp
from jax import lax
from jax.sharding import PartitionSpec as P

ITERS = 3

DIAG_SHIFT = 0.05
VISCOSITY = 0.5
GRAVITY = 0.1
GRADIENT_GAIN = 32.0

AXES = (("gx", 1), ("gy", 2), ("gz", 3))


def with_halo(cells, sides, width):
    for axis, dim in sides:
        count = lax.axis_size(axis)
        ends = count - 1
        head = lax.slice_in_dim(cells, 0, width, axis=dim)
        tail = lax.slice_in_dim(cells, cells.shape[dim] - width, cells.shape[dim], axis=dim)
        if count == 2:
            first = lax.axis_index(axis) == 0
            got = lax.ppermute(jnp.where(first, tail, head), axis, [(0, 1), (1, 0)])
            empty = jnp.zeros_like(got)
            cells = jnp.concatenate(
                [jnp.where(first, empty, got), cells, jnp.where(first, got, empty)], axis=dim
            )
            continue
        cells = jnp.concatenate(
            [
                lax.ppermute(tail, axis, [(i, (i + 1) % count) for i in range(ends)]),
                cells,
                lax.ppermute(head, axis, [((i + 1) % count, i) for i in range(ends)]),
            ],
            axis=dim,
        )
    return cells


def gather_rim(cells):
    comps, size_x, size_y, size_z, width = cells.shape
    counts = [lax.axis_size(axis) for axis, _ in AXES]
    devices = counts[0] * counts[1] * counts[2]
    rows = jnp.broadcast_to(cells[None], (devices,) + cells.shape)
    got = lax.all_to_all(rows, ("gx", "gy", "gz"), 0, 0, tiled=True)
    grid = got.reshape(counts[0], counts[1], counts[2], comps, size_x, size_y, size_z, width)
    grid = grid.transpose(3, 0, 4, 1, 5, 2, 6, 7).reshape(
        comps, counts[0] * size_x, counts[1] * size_y, counts[2] * size_z, width
    )
    padded = jnp.pad(grid, ((0, 0), (1, 1), (1, 1), (1, 1), (0, 0)))
    start = (
        0,
        lax.axis_index("gx") * size_x,
        lax.axis_index("gy") * size_y,
        lax.axis_index("gz") * size_z,
        0,
    )
    return lax.dynamic_slice(padded, start, (comps, size_x + 2, size_y + 2, size_z + 2, width))


def total(values):
    counts = [lax.axis_size(axis) for axis, _ in AXES]
    devices = counts[0] * counts[1] * counts[2]
    rows = jnp.broadcast_to(values[None], (devices,) + values.shape)
    got = lax.all_to_all(rows, ("gx", "gy", "gz"), 0, 0, tiled=True)
    return jnp.sum(got, axis=0)


def total_butterfly(values):
    for axis in ("gx", "gy", "gz"):
        count = lax.axis_size(axis)
        if count & (count - 1):
            values = lax.psum(values, axis)
            continue
        step = 1
        while step < count:
            values = values + lax.ppermute(values, axis, [(i, i ^ step) for i in range(count)])
            step *= 2
    return values


def neighbours(rim):
    comps, size_x, size_y, size_z, width = rim.shape
    blocks = []
    for ax in range(size_x - 2):
        for ay in range(size_y - 2):
            for az in range(size_z - 2):
                window = rim[:, ax:ax + 3, ay:ay + 3, az:az + 3, :]
                blocks.append(window.reshape(comps, 27 * width))
    return jnp.stack(blocks, axis=1)


def flat(cells):
    return cells.reshape(cells.shape[0], -1, cells.shape[4])


def wsum(weight, near):
    return jnp.sum(weight[None] * near[:, :, None, :], axis=-1)


def tile_corners(block_shape):
    _, size_x, size_y, size_z, _ = block_shape
    base = (
        lax.axis_index("gx") * size_x,
        lax.axis_index("gy") * size_y,
        lax.axis_index("gz") * size_z,
    )
    corners = []
    for ax in range(size_x):
        for ay in range(size_y):
            for az in range(size_z):
                corners.append(jnp.stack([base[0] + ax, base[1] + ay, base[2] + az]))
    return jnp.stack(corners, axis=1).astype(jnp.float32)


def adjacency(block_shape):
    _, size_x, size_y, size_z, width = block_shape
    rows = []
    for ax in range(size_x):
        for ay in range(size_y):
            for az in range(size_z):
                near = np.zeros((size_x + 2, size_y + 2, size_z + 2), np.float32)
                near[ax:ax + 3, ay:ay + 3, az:az + 3] = 1.0
                rows.append(np.repeat(near.reshape(-1), width))
    return np.stack(rows)


def solve3(matrix, rhs):
    h = [[matrix[i, j] for j in range(3)] for i in range(3)]
    g = [rhs[i] for i in range(3)]
    m1 = h[1][0] / h[0][0]
    m2 = h[2][0] / h[0][0]
    a11 = h[1][1] - m1 * h[0][1]
    a12 = h[1][2] - m1 * h[0][2]
    b1 = g[1] - m1 * g[0]
    a21 = h[2][1] - m2 * h[0][1]
    a22 = h[2][2] - m2 * h[0][2]
    b2 = g[2] - m2 * g[0]
    m3 = a21 / a11
    y2 = (b2 - m3 * b1) / (a22 - m3 * a12)
    y1 = (b1 - a12 * y2) / a11
    y0 = (g[0] - h[0][1] * y1 - h[0][2] * y2) / h[0][0]
    return (y0, y1, y2)


def on_device(positions, velocity, counts):
    block_shape = positions.shape
    width = positions.shape[4]
    slot_ids = jnp.arange(width, dtype=jnp.int32)
    valid_mask = (slot_ids[None, None, None, :] < counts[:, :, :, None]).astype(jnp.float32)[None]
    packed = jnp.concatenate([positions, valid_mask, velocity], axis=0)

    def rim_flat(cells):
        rim = gather_rim(cells)
        return rim.reshape(rim.shape[0], 1, -1)

    near_all = rim_flat(packed)
    near_x = near_all[0:3]
    near_valid = near_all[3]
    near_v = near_all[4:7]
    own_x = flat(positions)
    own_valid = flat(valid_mask)[0]
    own_v = flat(velocity)
    tiles = own_x.shape[1]

    offset = own_x[:, :, :, None] - near_x[:, :, None, :]
    distance = offset[0] * offset[0] + offset[1] * offset[1] + offset[2] * offset[2]
    closeness = jnp.maximum(1.0 - distance, 0.0)
    weight = (
        closeness * closeness * own_valid[:, :, None] * near_valid[:, None, :]
    ) * jnp.asarray(adjacency(block_shape))[:, None, :]

    corner = tile_corners(block_shape)[:, :, None]
    local_own = own_x - corner
    local_near = near_x - corner

    def spread_t(near_field):
        return jnp.broadcast_to(near_field, (near_field.shape[0], tiles, near_field.shape[2]))

    row = jnp.sum(weight, axis=-1)[None]
    sums = wsum(weight, jnp.concatenate([spread_t(near_v), local_near], axis=0))
    near_sums = sums[0:3]
    lever = local_own * row - sums[3:6]

    gravity_pull = jnp.array([0.0, 0.0, -GRAVITY], jnp.float32).reshape(3, 1, 1)
    predicted = own_valid[None] * (
        own_v + VISCOSITY / width * (near_sums - row * own_v) + gravity_pull
    )
    diagonal = DIAG_SHIFT + row / width

    def shaped(values):
        return values.reshape(values.shape[0], *block_shape[1:])

    near_pred = rim_flat(shaped(predicted))
    dotted = jnp.sum(near_pred * local_near, axis=0, keepdims=True)
    psums = wsum(weight, jnp.concatenate([spread_t(near_pred), dotted], axis=0))
    flux = jnp.sum(local_own * psums[0:3], axis=0, keepdims=True) - psums[3:4]
    source = -(GRADIENT_GAIN / width) * (
        jnp.sum(predicted * lever, axis=0, keepdims=True) - flux
    )

    basis = [source / diagonal]
    near_w = []
    near_wx = []
    for _ in range(ITERS):
        near_u = rim_flat(shaped(basis[-1]))
        out = wsum(weight, jnp.concatenate([spread_t(near_u), near_u * local_near], axis=0))
        near_w.append(out[0:1])
        near_wx.append(out[1:4])
        basis.append(-(out[0:1] / width) / diagonal)
    stacked = jnp.concatenate(basis, axis=0)
    weighted = stacked[:ITERS] * diagonal
    gram = total(jnp.sum(weighted[:, None] * stacked[None, :], axis=2))
    shift = width // 2
    while shift >= 1:
        gram = gram + jnp.roll(gram, shift, axis=-1)
        shift //= 2
    coords = solve3(gram[:, :ITERS] + gram[:, 1:], gram[:, 0])

    pressure = coords[0] * basis[0]
    applied = coords[0] * near_w[0]
    applied_x = coords[0] * near_wx[0]
    for k in range(1, ITERS):
        pressure = pressure + coords[k] * basis[k]
        applied = applied + coords[k] * near_w[k]
        applied_x = applied_x + coords[k] * near_wx[k]
    moments = local_own * applied - applied_x
    velocity_new = predicted - GRADIENT_GAIN / width * (pressure * lever - moments)
    return (shaped(velocity_new), shaped(pressure)[0])


def solution(mesh):
    in_specs = (
        P(None, "gx", "gy", "gz", None),
        P(None, "gx", "gy", "gz", None),
        P("gx", "gy", "gz"),
    )
    out_specs = (P(None, "gx", "gy", "gz", None), P("gx", "gy", "gz", None))
    return jax.shard_map(
        on_device, mesh=mesh, in_specs=in_specs, out_specs=out_specs, check_vma=False
    )
```

```python
import jax
import numpy as np
import jax.numpy as jnp
from jax import lax
from jax.sharding import PartitionSpec as P

ITERS = 3

DIAG_SHIFT = 0.05
VISCOSITY = 0.5
GRAVITY = 0.1
GRADIENT_GAIN = 32.0

AXES = (("gx", 1), ("gy", 2), ("gz", 3))


def with_halo(cells, sides, width):
    for axis, dim in sides:
        count = lax.axis_size(axis)
        ends = count - 1
        head = lax.slice_in_dim(cells, 0, width, axis=dim)
        tail = lax.slice_in_dim(cells, cells.shape[dim] - width, cells.shape[dim], axis=dim)
        if count == 2:
            first = lax.axis_index(axis) == 0
            got = lax.ppermute(jnp.where(first, tail, head), axis, [(0, 1), (1, 0)])
            empty = jnp.zeros_like(got)
            cells = jnp.concatenate(
                [jnp.where(first, empty, got), cells, jnp.where(first, got, empty)], axis=dim
            )
            continue
        cells = jnp.concatenate(
            [
                lax.ppermute(tail, axis, [(i, (i + 1) % count) for i in range(ends)]),
                cells,
                lax.ppermute(head, axis, [((i + 1) % count, i) for i in range(ends)]),
            ],
            axis=dim,
        )
    return cells


def gather_rim(cells):
    comps, size_x, size_y, size_z, width = cells.shape
    counts = [lax.axis_size(axis) for axis, _ in AXES]
    devices = counts[0] * counts[1] * counts[2]
    rows = jnp.broadcast_to(cells[None], (devices,) + cells.shape)
    got = lax.all_to_all(rows, ("gx", "gy", "gz"), 0, 0, tiled=True)
    grid = got.reshape(counts[0], counts[1], counts[2], comps, size_x, size_y, size_z, width)
    grid = grid.transpose(3, 0, 4, 1, 5, 2, 6, 7).reshape(
        comps, counts[0] * size_x, counts[1] * size_y, counts[2] * size_z, width
    )
    padded = jnp.pad(grid, ((0, 0), (1, 1), (1, 1), (1, 1), (0, 0)))
    start = (
        0,
        lax.axis_index("gx") * size_x,
        lax.axis_index("gy") * size_y,
        lax.axis_index("gz") * size_z,
        0,
    )
    return lax.dynamic_slice(padded, start, (comps, size_x + 2, size_y + 2, size_z + 2, width))


def total(values):
    counts = [lax.axis_size(axis) for axis, _ in AXES]
    devices = counts[0] * counts[1] * counts[2]
    rows = jnp.broadcast_to(values[None], (devices,) + values.shape)
    got = lax.all_to_all(rows, ("gx", "gy", "gz"), 0, 0, tiled=True)
    return jnp.sum(got, axis=0)


def total_butterfly(values):
    for axis in ("gx", "gy", "gz"):
        count = lax.axis_size(axis)
        if count & (count - 1):
            values = lax.psum(values, axis)
            continue
        step = 1
        while step < count:
            values = values + lax.ppermute(values, axis, [(i, i ^ step) for i in range(count)])
            step *= 2
    return values


def neighbours(rim):
    comps, size_x, size_y, size_z, width = rim.shape
    blocks = []
    for ax in range(size_x - 2):
        for ay in range(size_y - 2):
            for az in range(size_z - 2):
                window = rim[:, ax:ax + 3, ay:ay + 3, az:az + 3, :]
                blocks.append(window.reshape(comps, 27 * width))
    return jnp.stack(blocks, axis=1)


def flat(cells):
    return cells.reshape(cells.shape[0], -1, cells.shape[4])


def wsum(weight, near):
    return jnp.sum(weight[None] * near[:, :, None, :], axis=-1)


def tile_corners(block_shape):
    _, size_x, size_y, size_z, _ = block_shape
    base = (
        lax.axis_index("gx") * size_x,
        lax.axis_index("gy") * size_y,
        lax.axis_index("gz") * size_z,
    )
    corners = []
    for ax in range(size_x):
        for ay in range(size_y):
            for az in range(size_z):
                corners.append(jnp.stack([base[0] + ax, base[1] + ay, base[2] + az]))
    return jnp.stack(corners, axis=1).astype(jnp.float32)


def adjacency(block_shape):
    _, size_x, size_y, size_z, width = block_shape
    rows = []
    for ax in range(size_x):
        for ay in range(size_y):
            for az in range(size_z):
                near = np.zeros((size_x + 2, size_y + 2, size_z + 2), np.float32)
                near[ax:ax + 3, ay:ay + 3, az:az + 3] = 1.0
                rows.append(np.repeat(near.reshape(-1), width))
    return np.stack(rows)


def solve3(matrix, rhs):
    h = [[matrix[i, j] for j in range(3)] for i in range(3)]
    g = [rhs[i] for i in range(3)]
    m1 = h[1][0] / h[0][0]
    m2 = h[2][0] / h[0][0]
    a11 = h[1][1] - m1 * h[0][1]
    a12 = h[1][2] - m1 * h[0][2]
    b1 = g[1] - m1 * g[0]
    a21 = h[2][1] - m2 * h[0][1]
    a22 = h[2][2] - m2 * h[0][2]
    b2 = g[2] - m2 * g[0]
    m3 = a21 / a11
    y2 = (b2 - m3 * b1) / (a22 - m3 * a12)
    y1 = (b1 - a12 * y2) / a11
    y0 = (g[0] - h[0][1] * y1 - h[0][2] * y2) / h[0][0]
    return (y0, y1, y2)


def on_device(positions, velocity, counts):
    block_shape = positions.shape
    width = positions.shape[4]
    slot_ids = jnp.arange(width, dtype=jnp.int32)
    valid_mask = (slot_ids[None, None, None, :] < counts[:, :, :, None]).astype(jnp.float32)[None]
    packed = jnp.concatenate([positions, valid_mask, velocity], axis=0)

    def rim_flat(cells):
        rim = gather_rim(cells)
        return rim.reshape(rim.shape[0], 1, -1)

    near_all = rim_flat(packed)
    near_x = near_all[0:3]
    near_valid = near_all[3]
    near_v = near_all[4:7]
    own_x = flat(positions)
    own_valid = flat(valid_mask)[0]
    own_v = flat(velocity)
    tiles = own_x.shape[1]

    gaps = [own_x[k][:, :, None] - near_x[k][:, None, :] for k in range(3)]
    distance = gaps[0] * gaps[0] + gaps[1] * gaps[1] + gaps[2] * gaps[2]
    closeness = jnp.maximum(1.0 - distance, 0.0)
    weight = (
        closeness * closeness * own_valid[:, :, None] * near_valid[:, None, :]
    ) * jnp.asarray(adjacency(block_shape))[:, None, :]

    corner = tile_corners(block_shape)[:, :, None]
    local_own = own_x - corner
    local_near = near_x - corner

    def spread_t(near_field):
        return jnp.broadcast_to(near_field, (near_field.shape[0], tiles, near_field.shape[2]))

    row = jnp.sum(weight, axis=-1)[None]
    sums = wsum(weight, jnp.concatenate([spread_t(near_v), local_near], axis=0))
    near_sums = sums[0:3]
    lever = local_own * row - sums[3:6]

    gravity_pull = jnp.array([0.0, 0.0, -GRAVITY], jnp.float32).reshape(3, 1, 1)
    predicted = own_valid[None] * (
        own_v + VISCOSITY / width * (near_sums - row * own_v) + gravity_pull
    )
    diagonal = DIAG_SHIFT + row / width

    def shaped(values):
        return values.reshape(values.shape[0], *block_shape[1:])

    near_pred = rim_flat(shaped(predicted))
    dotted = jnp.sum(near_pred * local_near, axis=0, keepdims=True)
    psums = wsum(weight, jnp.concatenate([spread_t(near_pred), dotted], axis=0))
    flux = jnp.sum(local_own * psums[0:3], axis=0, keepdims=True) - psums[3:4]
    source = -(GRADIENT_GAIN / width) * (
        jnp.sum(predicted * lever, axis=0, keepdims=True) - flux
    )

    basis = [source / diagonal]
    near_w = []
    near_wx = []
    for _ in range(ITERS):
        near_u = rim_flat(shaped(basis[-1]))
        out = wsum(weight, jnp.concatenate([spread_t(near_u), near_u * local_near], axis=0))
        near_w.append(out[0:1])
        near_wx.append(out[1:4])
        basis.append(-(out[0:1] / width) / diagonal)
    stacked = jnp.concatenate(basis, axis=0)
    weighted = stacked[:ITERS] * diagonal
    gram = total(jnp.sum(weighted[:, None] * stacked[None, :], axis=2))
    shift = width // 2
    while shift >= 1:
        gram = gram + jnp.roll(gram, shift, axis=-1)
        shift //= 2
    coords = solve3(gram[:, :ITERS] + gram[:, 1:], gram[:, 0])

    pressure = coords[0] * basis[0]
    applied = coords[0] * near_w[0]
    applied_x = coords[0] * near_wx[0]
    for k in range(1, ITERS):
        pressure = pressure + coords[k] * basis[k]
        applied = applied + coords[k] * near_w[k]
        applied_x = applied_x + coords[k] * near_wx[k]
    moments = local_own * applied - applied_x
    velocity_new = predicted - GRADIENT_GAIN / width * (pressure * lever - moments)
    return (shaped(velocity_new), shaped(pressure)[0])


def solution(mesh):
    in_specs = (
        P(None, "gx", "gy", "gz", None),
        P(None, "gx", "gy", "gz", None),
        P("gx", "gy", "gz"),
    )
    out_specs = (P(None, "gx", "gy", "gz", None), P("gx", "gy", "gz", None))
    return jax.shard_map(
        on_device, mesh=mesh, in_specs=in_specs, out_specs=out_specs, check_vma=False
    )
```

```python
import jax
import jax.numpy as jnp
from jax import lax
from jax.sharding import PartitionSpec as P

ITERS = 3

DIAG_SHIFT = 0.05
VISCOSITY = 0.5
GRAVITY = 0.1
GRADIENT_GAIN = 32.0

AXES = (("gx", 1), ("gy", 2), ("gz", 3))


def with_halo(cells, sides, width):
    for axis, dim in sides:
        count = lax.axis_size(axis)
        ends = count - 1
        head = lax.slice_in_dim(cells, 0, width, axis=dim)
        tail = lax.slice_in_dim(cells, cells.shape[dim] - width, cells.shape[dim], axis=dim)
        if count == 2:
            first = lax.axis_index(axis) == 0
            got = lax.ppermute(jnp.where(first, tail, head), axis, [(0, 1), (1, 0)])
            empty = jnp.zeros_like(got)
            cells = jnp.concatenate(
                [jnp.where(first, empty, got), cells, jnp.where(first, got, empty)], axis=dim
            )
            continue
        cells = jnp.concatenate(
            [
                lax.ppermute(tail, axis, [(i, (i + 1) % count) for i in range(ends)]),
                cells,
                lax.ppermute(head, axis, [((i + 1) % count, i) for i in range(ends)]),
            ],
            axis=dim,
        )
    return cells


def gather_rim(cells):
    comps, size_x, size_y, size_z, width = cells.shape
    counts = [lax.axis_size(axis) for axis, _ in AXES]
    devices = counts[0] * counts[1] * counts[2]
    rows = jnp.broadcast_to(cells[None], (devices,) + cells.shape)
    got = lax.all_to_all(rows, ("gx", "gy", "gz"), 0, 0, tiled=True)
    grid = got.reshape(counts[0], counts[1], counts[2], comps, size_x, size_y, size_z, width)
    grid = grid.transpose(3, 2, 6, 0, 4, 1, 5, 7).reshape(
        comps, counts[2] * size_z, counts[0] * size_x, counts[1] * size_y, width
    )
    padded = jnp.pad(grid, ((0, 0), (1, 1), (1, 1), (1, 1), (0, 0)))
    start = (
        0,
        lax.axis_index("gz") * size_z,
        lax.axis_index("gx") * size_x,
        lax.axis_index("gy") * size_y,
        0,
    )
    return lax.dynamic_slice(padded, start, (comps, size_z + 2, size_x + 2, size_y + 2, width))


def total(values):
    counts = [lax.axis_size(axis) for axis, _ in AXES]
    devices = counts[0] * counts[1] * counts[2]
    rows = jnp.broadcast_to(values[None], (devices,) + values.shape)
    got = lax.all_to_all(rows, ("gx", "gy", "gz"), 0, 0, tiled=True)
    return jnp.sum(got, axis=0)


def total_butterfly(values):
    for axis in ("gx", "gy", "gz"):
        count = lax.axis_size(axis)
        if count & (count - 1):
            values = lax.psum(values, axis)
            continue
        step = 1
        while step < count:
            values = values + lax.ppermute(values, axis, [(i, i ^ step) for i in range(count)])
            step *= 2
    return values


def neighbours(rim):
    comps, size_z, size_x, size_y, width = rim.shape
    blocks = []
    for ax in range(size_x - 2):
        for ay in range(size_y - 2):
            for az in range(size_z - 2):
                window = rim[:, az:az + 3, ax:ax + 3, ay:ay + 3, :]
                blocks.append(window.reshape(comps, 27 * width))
    return jnp.stack(blocks, axis=1)


def flat(cells):
    return cells.reshape(cells.shape[0], -1, cells.shape[4])


def wsum(weight, near):
    return jnp.sum(weight[None] * near[:, :, None, :], axis=-1)


def tile_corners(block_shape):
    _, size_x, size_y, size_z, _ = block_shape
    base = (
        lax.axis_index("gx") * size_x,
        lax.axis_index("gy") * size_y,
        lax.axis_index("gz") * size_z,
    )
    corners = []
    for ax in range(size_x):
        for ay in range(size_y):
            for az in range(size_z):
                corners.append(jnp.stack([base[0] + ax, base[1] + ay, base[2] + az]))
    return jnp.stack(corners, axis=1).astype(jnp.float32)


def solve3(matrix, rhs):
    h = [[matrix[i, j] for j in range(3)] for i in range(3)]
    g = [rhs[i] for i in range(3)]
    m1 = h[1][0] / h[0][0]
    m2 = h[2][0] / h[0][0]
    a11 = h[1][1] - m1 * h[0][1]
    a12 = h[1][2] - m1 * h[0][2]
    b1 = g[1] - m1 * g[0]
    a21 = h[2][1] - m2 * h[0][1]
    a22 = h[2][2] - m2 * h[0][2]
    b2 = g[2] - m2 * g[0]
    m3 = a21 / a11
    y2 = (b2 - m3 * b1) / (a22 - m3 * a12)
    y1 = (b1 - a12 * y2) / a11
    y0 = (g[0] - h[0][1] * y1 - h[0][2] * y2) / h[0][0]
    return (y0, y1, y2)


def on_device(positions, velocity, counts):
    block_shape = positions.shape
    width = positions.shape[4]
    slot_ids = jnp.arange(width, dtype=jnp.int32)
    valid_mask = (slot_ids[None, None, None, :] < counts[:, :, :, None]).astype(jnp.float32)[None]
    packed = jnp.concatenate([positions, valid_mask, velocity], axis=0)

    def rim_flat(cells):
        return neighbours(gather_rim(cells))

    near_all = rim_flat(packed)
    near_x = near_all[0:3]
    near_valid = near_all[3]
    near_v = near_all[4:7]
    own_x = flat(positions)
    own_valid = flat(valid_mask)[0]
    own_v = flat(velocity)

    gaps = [own_x[k][:, :, None] - near_x[k][:, None, :] for k in range(3)]
    distance = gaps[0] * gaps[0] + gaps[1] * gaps[1] + gaps[2] * gaps[2]
    closeness = jnp.maximum(1.0 - distance, 0.0)
    weight = closeness * closeness * own_valid[:, :, None] * near_valid[:, None, :]

    corner = tile_corners(block_shape)[:, :, None]
    local_own = own_x - corner
    local_near = near_x - corner

    row = jnp.sum(weight, axis=-1)[None]
    sums = wsum(weight, jnp.concatenate([near_v, local_near], axis=0))
    near_sums = sums[0:3]
    lever = local_own * row - sums[3:6]

    gravity_pull = jnp.array([0.0, 0.0, -GRAVITY], jnp.float32).reshape(3, 1, 1)
    predicted = own_valid[None] * (
        own_v + VISCOSITY / width * (near_sums - row * own_v) + gravity_pull
    )
    diagonal = DIAG_SHIFT + row / width

    def shaped(values):
        return values.reshape(values.shape[0], *block_shape[1:])

    near_pred = rim_flat(shaped(predicted))
    dotted = jnp.sum(near_pred * local_near, axis=0, keepdims=True)
    psums = wsum(weight, jnp.concatenate([near_pred, dotted], axis=0))
    flux = jnp.sum(local_own * psums[0:3], axis=0, keepdims=True) - psums[3:4]
    source = -(GRADIENT_GAIN / width) * (
        jnp.sum(predicted * lever, axis=0, keepdims=True) - flux
    )

    basis = [source / diagonal]
    near_w = []
    near_wx = []
    for _ in range(ITERS):
        near_u = rim_flat(shaped(basis[-1]))
        out = wsum(weight, jnp.concatenate([near_u, near_u * local_near], axis=0))
        near_w.append(out[0:1])
        near_wx.append(out[1:4])
        basis.append(-(out[0:1] / width) / diagonal)
    stacked = jnp.concatenate(basis, axis=0)
    weighted = stacked[:ITERS] * diagonal
    gram = total(jnp.sum(weighted[:, None] * stacked[None, :], axis=2))
    shift = width // 2
    while shift >= 1:
        gram = gram + jnp.roll(gram, shift, axis=-1)
        shift //= 2
    coords = solve3(gram[:, :ITERS] + gram[:, 1:], gram[:, 0])

    pressure = coords[0] * basis[0]
    applied = coords[0] * near_w[0]
    applied_x = coords[0] * near_wx[0]
    for k in range(1, ITERS):
        pressure = pressure + coords[k] * basis[k]
        applied = applied + coords[k] * near_w[k]
        applied_x = applied_x + coords[k] * near_wx[k]
    moments = local_own * applied - applied_x
    velocity_new = predicted - GRADIENT_GAIN / width * (pressure * lever - moments)
    return (shaped(velocity_new), shaped(pressure)[0])


def solution(mesh):
    in_specs = (
        P(None, "gx", "gy", "gz", None),
        P(None, "gx", "gy", "gz", None),
        P("gx", "gy", "gz"),
    )
    out_specs = (P(None, "gx", "gy", "gz", None), P("gx", "gy", "gz", None))
    return jax.shard_map(
        on_device, mesh=mesh, in_specs=in_specs, out_specs=out_specs, check_vma=False
    )
```

```python
import jax
import jax.numpy as jnp
from jax import lax
from jax.sharding import PartitionSpec as P

ITERS = 3

DIAG_SHIFT = 0.05
VISCOSITY = 0.5
GRAVITY = 0.1
GRADIENT_GAIN = 32.0

AXES = (("gx", 1), ("gy", 2), ("gz", 3))


def with_halo(cells, sides, width):
    for axis, dim in sides:
        count = lax.axis_size(axis)
        ends = count - 1
        head = lax.slice_in_dim(cells, 0, width, axis=dim)
        tail = lax.slice_in_dim(cells, cells.shape[dim] - width, cells.shape[dim], axis=dim)
        if count == 2:
            first = lax.axis_index(axis) == 0
            got = lax.ppermute(jnp.where(first, tail, head), axis, [(0, 1), (1, 0)])
            empty = jnp.zeros_like(got)
            cells = jnp.concatenate(
                [jnp.where(first, empty, got), cells, jnp.where(first, got, empty)], axis=dim
            )
            continue
        cells = jnp.concatenate(
            [
                lax.ppermute(tail, axis, [(i, (i + 1) % count) for i in range(ends)]),
                cells,
                lax.ppermute(head, axis, [((i + 1) % count, i) for i in range(ends)]),
            ],
            axis=dim,
        )
    return cells


def gather_rim(cells):
    comps, size_x, size_y, size_z, width = cells.shape
    counts = [lax.axis_size(axis) for axis, _ in AXES]
    devices = counts[0] * counts[1] * counts[2]
    rows = jnp.broadcast_to(cells[None], (devices,) + cells.shape)
    got = lax.all_to_all(rows, ("gx", "gy", "gz"), 0, 0, tiled=True)
    grid = got.reshape(counts[0], counts[1], counts[2], comps, size_x, size_y, size_z, width)
    grid = grid.transpose(3, 2, 6, 0, 4, 1, 5, 7).reshape(
        comps, counts[2] * size_z, counts[0] * size_x, counts[1] * size_y, width
    )
    padded = jnp.pad(grid, ((0, 0), (1, 1), (1, 1), (1, 1), (0, 0)))
    start = (
        0,
        lax.axis_index("gz") * size_z,
        lax.axis_index("gx") * size_x,
        lax.axis_index("gy") * size_y,
        0,
    )
    return lax.dynamic_slice(padded, start, (comps, size_z + 2, size_x + 2, size_y + 2, width))


def total(values):
    counts = [lax.axis_size(axis) for axis, _ in AXES]
    devices = counts[0] * counts[1] * counts[2]
    rows = jnp.broadcast_to(values[None], (devices,) + values.shape)
    got = lax.all_to_all(rows, ("gx", "gy", "gz"), 0, 0, tiled=True)
    return jnp.sum(got, axis=0)


def total_butterfly(values):
    for axis in ("gx", "gy", "gz"):
        count = lax.axis_size(axis)
        if count & (count - 1):
            values = lax.psum(values, axis)
            continue
        step = 1
        while step < count:
            values = values + lax.ppermute(values, axis, [(i, i ^ step) for i in range(count)])
            step *= 2
    return values


def neighbours(rim):
    comps, size_z, size_x, size_y, width = rim.shape
    blocks = []
    for ax in range(size_x - 2):
        for ay in range(size_y - 2):
            for az in range(size_z - 2):
                window = rim[:, az:az + 3, ax:ax + 3, ay:ay + 3, :]
                blocks.append(window.reshape(comps, 27 * width))
    return blocks


def flat(cells):
    return cells.reshape(cells.shape[0], -1, cells.shape[4])


def wsum(weight, near):
    return jnp.stack(
        [jnp.sum(tile_weight[None] * tile_near[:, None, :], axis=-1) for tile_weight, tile_near in zip(weight, near)],
        axis=1,
    )


def tile_corners(block_shape):
    _, size_x, size_y, size_z, _ = block_shape
    base = (
        lax.axis_index("gx") * size_x,
        lax.axis_index("gy") * size_y,
        lax.axis_index("gz") * size_z,
    )
    corners = []
    for ax in range(size_x):
        for ay in range(size_y):
            for az in range(size_z):
                corners.append(jnp.stack([base[0] + ax, base[1] + ay, base[2] + az]))
    return jnp.stack(corners, axis=1).astype(jnp.float32)


def solve3(matrix, rhs):
    h = [[matrix[i, j] for j in range(3)] for i in range(3)]
    g = [rhs[i] for i in range(3)]
    m1 = h[1][0] / h[0][0]
    m2 = h[2][0] / h[0][0]
    a11 = h[1][1] - m1 * h[0][1]
    a12 = h[1][2] - m1 * h[0][2]
    b1 = g[1] - m1 * g[0]
    a21 = h[2][1] - m2 * h[0][1]
    a22 = h[2][2] - m2 * h[0][2]
    b2 = g[2] - m2 * g[0]
    m3 = a21 / a11
    y2 = (b2 - m3 * b1) / (a22 - m3 * a12)
    y1 = (b1 - a12 * y2) / a11
    y0 = (g[0] - h[0][1] * y1 - h[0][2] * y2) / h[0][0]
    return (y0, y1, y2)


def on_device(positions, velocity, counts):
    block_shape = positions.shape
    width = positions.shape[4]
    slot_ids = jnp.arange(width, dtype=jnp.int32)
    valid_mask = (slot_ids[None, None, None, :] < counts[:, :, :, None]).astype(jnp.float32)[None]
    packed = jnp.concatenate([positions, valid_mask, velocity], axis=0)

    def rim_flat(cells):
        return neighbours(gather_rim(cells))

    near_all = rim_flat(packed)
    own_x = flat(positions)
    own_valid = flat(valid_mask)[0]
    own_v = flat(velocity)
    corner = tile_corners(block_shape)

    weight = []
    local_near = []
    for t, tile in enumerate(near_all):
        gaps = [own_x[k, t][:, None] - tile[k][None, :] for k in range(3)]
        distance = gaps[0] * gaps[0] + gaps[1] * gaps[1] + gaps[2] * gaps[2]
        closeness = jnp.maximum(1.0 - distance, 0.0)
        weight.append(closeness * closeness * own_valid[t][:, None] * tile[3][None, :])
        local_near.append(tile[0:3] - corner[:, t][:, None])
    local_own = own_x - corner[:, :, None]

    row = jnp.stack([jnp.sum(tile_weight, axis=-1) for tile_weight in weight])[None]
    sums = wsum(weight, [jnp.concatenate([tile[4:7], near], axis=0) for tile, near in zip(near_all, local_near)])
    near_sums = sums[0:3]
    lever = local_own * row - sums[3:6]

    gravity_pull = jnp.array([0.0, 0.0, -GRAVITY], jnp.float32).reshape(3, 1, 1)
    predicted = own_valid[None] * (
        own_v + VISCOSITY / width * (near_sums - row * own_v) + gravity_pull
    )
    diagonal = DIAG_SHIFT + row / width

    def shaped(values):
        return values.reshape(values.shape[0], *block_shape[1:])

    near_pred = rim_flat(shaped(predicted))
    psums = wsum(
        weight,
        [
            jnp.concatenate([tile, jnp.sum(tile * near, axis=0, keepdims=True)], axis=0)
            for tile, near in zip(near_pred, local_near)
        ],
    )
    flux = jnp.sum(local_own * psums[0:3], axis=0, keepdims=True) - psums[3:4]
    source = -(GRADIENT_GAIN / width) * (
        jnp.sum(predicted * lever, axis=0, keepdims=True) - flux
    )

    basis = [source / diagonal]
    near_w = []
    near_wx = []
    for _ in range(ITERS):
        near_u = rim_flat(shaped(basis[-1]))
        out = wsum(weight, [jnp.concatenate([tile, tile * near], axis=0) for tile, near in zip(near_u, local_near)])
        near_w.append(out[0:1])
        near_wx.append(out[1:4])
        basis.append(-(out[0:1] / width) / diagonal)
    stacked = jnp.concatenate(basis, axis=0)
    weighted = stacked[:ITERS] * diagonal
    gram = total(jnp.sum(weighted[:, None] * stacked[None, :], axis=2))
    shift = width // 2
    while shift >= 1:
        gram = gram + jnp.roll(gram, shift, axis=-1)
        shift //= 2
    coords = solve3(gram[:, :ITERS] + gram[:, 1:], gram[:, 0])

    pressure = coords[0] * basis[0]
    applied = coords[0] * near_w[0]
    applied_x = coords[0] * near_wx[0]
    for k in range(1, ITERS):
        pressure = pressure + coords[k] * basis[k]
        applied = applied + coords[k] * near_w[k]
        applied_x = applied_x + coords[k] * near_wx[k]
    moments = local_own * applied - applied_x
    velocity_new = predicted - GRADIENT_GAIN / width * (pressure * lever - moments)
    return (shaped(velocity_new), shaped(pressure)[0])


def solution(mesh):
    in_specs = (
        P(None, "gx", "gy", "gz", None),
        P(None, "gx", "gy", "gz", None),
        P("gx", "gy", "gz"),
    )
    out_specs = (P(None, "gx", "gy", "gz", None), P("gx", "gy", "gz", None))
    return jax.shard_map(
        on_device, mesh=mesh, in_specs=in_specs, out_specs=out_specs, check_vma=False
    )
```

```python
import jax
import jax.numpy as jnp
from jax import lax
from jax.sharding import PartitionSpec as P

ITERS = 3

DIAG_SHIFT = 0.05
VISCOSITY = 0.5
GRAVITY = 0.1
GRADIENT_GAIN = 32.0

AXES = (("gx", 1), ("gy", 2), ("gz", 3))


def with_halo(cells, sides, width):
    for axis, dim in sides:
        count = lax.axis_size(axis)
        ends = count - 1
        head = lax.slice_in_dim(cells, 0, width, axis=dim)
        tail = lax.slice_in_dim(cells, cells.shape[dim] - width, cells.shape[dim], axis=dim)
        if count == 2:
            first = lax.axis_index(axis) == 0
            got = lax.ppermute(jnp.where(first, tail, head), axis, [(0, 1), (1, 0)])
            empty = jnp.zeros_like(got)
            cells = jnp.concatenate(
                [jnp.where(first, empty, got), cells, jnp.where(first, got, empty)], axis=dim
            )
            continue
        cells = jnp.concatenate(
            [
                lax.ppermute(tail, axis, [(i, (i + 1) % count) for i in range(ends)]),
                cells,
                lax.ppermute(head, axis, [((i + 1) % count, i) for i in range(ends)]),
            ],
            axis=dim,
        )
    return cells


def gather_rim(cells):
    comps, size_x, size_y, size_z, width = cells.shape
    counts = [lax.axis_size(axis) for axis, _ in AXES]
    devices = counts[0] * counts[1] * counts[2]
    rows = jnp.broadcast_to(cells[None], (devices,) + cells.shape)
    got = lax.all_to_all(rows, ("gx", "gy", "gz"), 0, 0, tiled=True)
    grid = got.reshape(counts[0], counts[1], counts[2], comps, size_x, size_y, size_z, width)
    grid = grid.transpose(3, 2, 6, 0, 4, 1, 5, 7).reshape(
        comps, counts[2] * size_z, counts[0] * size_x, counts[1] * size_y, width
    )
    padded = jnp.pad(grid, ((0, 0), (1, 1), (1, 1), (1, 1), (0, 0)))
    start = (
        0,
        lax.axis_index("gz") * size_z,
        lax.axis_index("gx") * size_x,
        lax.axis_index("gy") * size_y,
        0,
    )
    return lax.dynamic_slice(padded, start, (comps, size_z + 2, size_x + 2, size_y + 2, width))


def total(values):
    counts = [lax.axis_size(axis) for axis, _ in AXES]
    devices = counts[0] * counts[1] * counts[2]
    rows = jnp.broadcast_to(values[None], (devices,) + values.shape)
    got = lax.all_to_all(rows, ("gx", "gy", "gz"), 0, 0, tiled=True)
    return jnp.sum(got, axis=0)


def total_butterfly(values):
    for axis in ("gx", "gy", "gz"):
        count = lax.axis_size(axis)
        if count & (count - 1):
            values = lax.psum(values, axis)
            continue
        step = 1
        while step < count:
            values = values + lax.ppermute(values, axis, [(i, i ^ step) for i in range(count)])
            step *= 2
    return values


def neighbours(rim):
    comps, size_z, size_x, size_y, width = rim.shape
    if size_x == 3 and size_y == 3:
        slab = 9 * width
        flat_rim = rim.reshape(comps, size_z * slab)
        return [flat_rim[:, az * slab:(az + 3) * slab] for az in range(size_z - 2)]
    blocks = []
    for ax in range(size_x - 2):
        for ay in range(size_y - 2):
            for az in range(size_z - 2):
                window = rim[:, az:az + 3, ax:ax + 3, ay:ay + 3, :]
                blocks.append(window.reshape(comps, 27 * width))
    return blocks


def flat(cells):
    return cells.reshape(cells.shape[0], -1, cells.shape[4])


def wsum(weight, near):
    return jnp.stack(
        [jnp.sum(tile_weight[None] * tile_near[:, None, :], axis=-1) for tile_weight, tile_near in zip(weight, near)],
        axis=1,
    )


def tile_corners(block_shape):
    _, size_x, size_y, size_z, _ = block_shape
    base = (
        lax.axis_index("gx") * size_x,
        lax.axis_index("gy") * size_y,
        lax.axis_index("gz") * size_z,
    )
    corners = []
    for ax in range(size_x):
        for ay in range(size_y):
            for az in range(size_z):
                corners.append(jnp.stack([base[0] + ax, base[1] + ay, base[2] + az]))
    return jnp.stack(corners, axis=1).astype(jnp.float32)


def solve3(matrix, rhs):
    h = [[matrix[i, j] for j in range(3)] for i in range(3)]
    g = [rhs[i] for i in range(3)]
    m1 = h[1][0] / h[0][0]
    m2 = h[2][0] / h[0][0]
    a11 = h[1][1] - m1 * h[0][1]
    a12 = h[1][2] - m1 * h[0][2]
    b1 = g[1] - m1 * g[0]
    a21 = h[2][1] - m2 * h[0][1]
    a22 = h[2][2] - m2 * h[0][2]
    b2 = g[2] - m2 * g[0]
    m3 = a21 / a11
    y2 = (b2 - m3 * b1) / (a22 - m3 * a12)
    y1 = (b1 - a12 * y2) / a11
    y0 = (g[0] - h[0][1] * y1 - h[0][2] * y2) / h[0][0]
    return (y0, y1, y2)


def on_device(positions, velocity, counts):
    block_shape = positions.shape
    width = positions.shape[4]
    slot_ids = jnp.arange(width, dtype=jnp.int32)
    valid_mask = (slot_ids[None, None, None, :] < counts[:, :, :, None]).astype(jnp.float32)[None]
    packed = jnp.concatenate([positions, valid_mask, velocity], axis=0)

    def rim_flat(cells):
        return neighbours(gather_rim(cells))

    near_all = rim_flat(packed)
    own_x = flat(positions)
    own_valid = flat(valid_mask)[0]
    own_v = flat(velocity)
    corner = tile_corners(block_shape)

    weight = []
    local_near = []
    for t, tile in enumerate(near_all):
        gaps = [own_x[k, t][:, None] - tile[k][None, :] for k in range(3)]
        distance = gaps[0] * gaps[0] + gaps[1] * gaps[1] + gaps[2] * gaps[2]
        closeness = jnp.maximum(1.0 - distance, 0.0)
        weight.append(closeness * closeness * own_valid[t][:, None] * tile[3][None, :])
        local_near.append(tile[0:3] - corner[:, t][:, None])
    local_own = own_x - corner[:, :, None]

    row = jnp.stack([jnp.sum(tile_weight, axis=-1) for tile_weight in weight])[None]
    sums = wsum(weight, [jnp.concatenate([tile[4:7], near], axis=0) for tile, near in zip(near_all, local_near)])
    near_sums = sums[0:3]
    lever = local_own * row - sums[3:6]

    gravity_pull = jnp.array([0.0, 0.0, -GRAVITY], jnp.float32).reshape(3, 1, 1)
    predicted = own_valid[None] * (
        own_v + VISCOSITY / width * (near_sums - row * own_v) + gravity_pull
    )
    diagonal = DIAG_SHIFT + row / width

    def shaped(values):
        return values.reshape(values.shape[0], *block_shape[1:])

    near_pred = rim_flat(shaped(predicted))
    psums = wsum(
        weight,
        [
            jnp.concatenate([tile, jnp.sum(tile * near, axis=0, keepdims=True)], axis=0)
            for tile, near in zip(near_pred, local_near)
        ],
    )
    flux = jnp.sum(local_own * psums[0:3], axis=0, keepdims=True) - psums[3:4]
    source = -(GRADIENT_GAIN / width) * (
        jnp.sum(predicted * lever, axis=0, keepdims=True) - flux
    )

    basis = [source / diagonal]
    near_w = []
    near_wx = []
    for _ in range(ITERS):
        near_u = rim_flat(shaped(basis[-1]))
        out = wsum(weight, [jnp.concatenate([tile, tile * near], axis=0) for tile, near in zip(near_u, local_near)])
        near_w.append(out[0:1])
        near_wx.append(out[1:4])
        basis.append(-(out[0:1] / width) / diagonal)
    stacked = jnp.concatenate(basis, axis=0)
    weighted = stacked[:ITERS] * diagonal
    gram = total(jnp.sum(weighted[:, None] * stacked[None, :], axis=2))
    shift = width // 2
    while shift >= 1:
        gram = gram + jnp.roll(gram, shift, axis=-1)
        shift //= 2
    coords = solve3(gram[:, :ITERS] + gram[:, 1:], gram[:, 0])

    pressure = coords[0] * basis[0]
    applied = coords[0] * near_w[0]
    applied_x = coords[0] * near_wx[0]
    for k in range(1, ITERS):
        pressure = pressure + coords[k] * basis[k]
        applied = applied + coords[k] * near_w[k]
        applied_x = applied_x + coords[k] * near_wx[k]
    moments = local_own * applied - applied_x
    velocity_new = predicted - GRADIENT_GAIN / width * (pressure * lever - moments)
    return (shaped(velocity_new), shaped(pressure)[0])


def solution(mesh):
    in_specs = (
        P(None, "gx", "gy", "gz", None),
        P(None, "gx", "gy", "gz", None),
        P("gx", "gy", "gz"),
    )
    out_specs = (P(None, "gx", "gy", "gz", None), P("gx", "gy", "gz", None))
    return jax.shard_map(
        on_device, mesh=mesh, in_specs=in_specs, out_specs=out_specs, check_vma=False
    )
```

```python
import jax
import numpy as np
import jax.numpy as jnp
from jax import lax
from jax.sharding import PartitionSpec as P

ITERS = 3

DIAG_SHIFT = 0.05
VISCOSITY = 0.5
GRAVITY = 0.1
GRADIENT_GAIN = 32.0

AXES = (("gx", 1), ("gy", 2), ("gz", 3))


def with_halo(cells, sides, width):
    for axis, dim in sides:
        count = lax.axis_size(axis)
        ends = count - 1
        head = lax.slice_in_dim(cells, 0, width, axis=dim)
        tail = lax.slice_in_dim(cells, cells.shape[dim] - width, cells.shape[dim], axis=dim)
        if count == 2:
            first = lax.axis_index(axis) == 0
            got = lax.ppermute(jnp.where(first, tail, head), axis, [(0, 1), (1, 0)])
            empty = jnp.zeros_like(got)
            cells = jnp.concatenate(
                [jnp.where(first, empty, got), cells, jnp.where(first, got, empty)], axis=dim
            )
            continue
        cells = jnp.concatenate(
            [
                lax.ppermute(tail, axis, [(i, (i + 1) % count) for i in range(ends)]),
                cells,
                lax.ppermute(head, axis, [((i + 1) % count, i) for i in range(ends)]),
            ],
            axis=dim,
        )
    return cells


def gather_rim(cells):
    comps, size_x, size_y, size_z, width = cells.shape
    counts = [lax.axis_size(axis) for axis, _ in AXES]
    devices = counts[0] * counts[1] * counts[2]
    rows = jnp.broadcast_to(cells[None], (devices,) + cells.shape)
    got = lax.all_to_all(rows, ("gx", "gy", "gz"), 0, 0, tiled=True)
    grid = got.reshape(counts[0], counts[1], counts[2], comps, size_x, size_y, size_z, width)
    grid = grid.transpose(3, 0, 4, 1, 5, 2, 6, 7).reshape(
        comps, counts[0] * size_x, counts[1] * size_y, counts[2] * size_z, width
    )
    padded = jnp.pad(grid, ((0, 0), (1, 1), (1, 1), (1, 1), (0, 0)))
    start = (
        0,
        lax.axis_index("gx") * size_x,
        lax.axis_index("gy") * size_y,
        lax.axis_index("gz") * size_z,
        0,
    )
    return lax.dynamic_slice(padded, start, (comps, size_x + 2, size_y + 2, size_z + 2, width))


def total(values):
    counts = [lax.axis_size(axis) for axis, _ in AXES]
    devices = counts[0] * counts[1] * counts[2]
    rows = jnp.broadcast_to(values[None], (devices,) + values.shape)
    got = lax.all_to_all(rows, ("gx", "gy", "gz"), 0, 0, tiled=True)
    return jnp.sum(got, axis=0)


def total_butterfly(values):
    for axis in ("gx", "gy", "gz"):
        count = lax.axis_size(axis)
        if count & (count - 1):
            values = lax.psum(values, axis)
            continue
        step = 1
        while step < count:
            values = values + lax.ppermute(values, axis, [(i, i ^ step) for i in range(count)])
            step *= 2
    return values


def neighbours(rim):
    comps, size_x, size_y, size_z, width = rim.shape
    blocks = []
    for ax in range(size_x - 2):
        for ay in range(size_y - 2):
            for az in range(size_z - 2):
                window = rim[:, ax:ax + 3, ay:ay + 3, az:az + 3, :]
                blocks.append(window.reshape(comps, 27 * width))
    return jnp.stack(blocks, axis=1)


def flat(cells):
    return cells.reshape(cells.shape[0], -1, cells.shape[4])


def wsum(weight, near):
    return jnp.sum(weight[None] * near[:, :, None, :], axis=-1)


def tile_corners(block_shape):
    _, size_x, size_y, size_z, _ = block_shape
    base = (
        lax.axis_index("gx") * size_x,
        lax.axis_index("gy") * size_y,
        lax.axis_index("gz") * size_z,
    )
    corners = []
    for ax in range(size_x):
        for ay in range(size_y):
            for az in range(size_z):
                corners.append(jnp.stack([base[0] + ax, base[1] + ay, base[2] + az]))
    return jnp.stack(corners, axis=1).astype(jnp.float32)


def adjacency(block_shape):
    _, size_x, size_y, size_z, width = block_shape
    rows = []
    for ax in range(size_x):
        for ay in range(size_y):
            for az in range(size_z):
                near = np.zeros((size_x + 2, size_y + 2, size_z + 2), np.float32)
                near[ax:ax + 3, ay:ay + 3, az:az + 3] = 1.0
                rows.append(np.repeat(near.reshape(-1), width))
    return np.stack(rows)


def solve3(matrix, rhs):
    h = [[matrix[i, j] for j in range(3)] for i in range(3)]
    g = [rhs[i] for i in range(3)]
    m1 = h[1][0] / h[0][0]
    m2 = h[2][0] / h[0][0]
    a11 = h[1][1] - m1 * h[0][1]
    a12 = h[1][2] - m1 * h[0][2]
    b1 = g[1] - m1 * g[0]
    a21 = h[2][1] - m2 * h[0][1]
    a22 = h[2][2] - m2 * h[0][2]
    b2 = g[2] - m2 * g[0]
    m3 = a21 / a11
    y2 = (b2 - m3 * b1) / (a22 - m3 * a12)
    y1 = (b1 - a12 * y2) / a11
    y0 = (g[0] - h[0][1] * y1 - h[0][2] * y2) / h[0][0]
    return (y0, y1, y2)


def on_device(positions, velocity, counts):
    block_shape = positions.shape
    width = positions.shape[4]
    slot_ids = jnp.arange(width, dtype=jnp.int32)
    valid_mask = (slot_ids[None, None, None, :] < counts[:, :, :, None]).astype(jnp.float32)[None]
    packed = jnp.concatenate([positions, valid_mask, velocity], axis=0)

    def rim_flat(cells):
        rim = gather_rim(cells)
        return rim.reshape(rim.shape[0], 1, -1)

    near_all = rim_flat(packed)
    near_x = near_all[0:3]
    near_valid = near_all[3]
    near_v = near_all[4:7]
    own_x = flat(positions)
    own_valid = flat(valid_mask)[0]
    own_v = flat(velocity)
    tiles = own_x.shape[1]

    gaps = [own_x[k][:, :, None] - near_x[k][:, None, :] for k in range(3)]
    distance = gaps[0] * gaps[0] + gaps[1] * gaps[1] + gaps[2] * gaps[2]
    closeness = jnp.maximum(1.0 - distance, 0.0)
    weight = (
        closeness * closeness * own_valid[:, :, None] * near_valid[:, None, :]
    ) * jnp.asarray(adjacency(block_shape))[:, None, :]

    corner = tile_corners(block_shape)[:, :, None]
    local_own = own_x - corner
    local_near = near_x - corner

    def spread_t(near_field):
        return jnp.broadcast_to(near_field, (near_field.shape[0], tiles, near_field.shape[2]))

    row = jnp.sum(weight, axis=-1)[None]
    fields = [near_v[k] for k in range(3)] + [local_near[k] for k in range(3)]
    sums = jnp.stack([jnp.sum(weight * field[:, None, :], axis=-1) for field in fields])
    near_sums = sums[0:3]
    lever = local_own * row - sums[3:6]

    gravity_pull = jnp.array([0.0, 0.0, -GRAVITY], jnp.float32).reshape(3, 1, 1)
    predicted = own_valid[None] * (
        own_v + VISCOSITY / width * (near_sums - row * own_v) + gravity_pull
    )
    diagonal = DIAG_SHIFT + row / width

    def shaped(values):
        return values.reshape(values.shape[0], *block_shape[1:])

    near_pred = rim_flat(shaped(predicted))
    dotted = jnp.sum(near_pred * local_near, axis=0, keepdims=True)
    psums = wsum(weight, jnp.concatenate([spread_t(near_pred), dotted], axis=0))
    flux = jnp.sum(local_own * psums[0:3], axis=0, keepdims=True) - psums[3:4]
    source = -(GRADIENT_GAIN / width) * (
        jnp.sum(predicted * lever, axis=0, keepdims=True) - flux
    )

    basis = [source / diagonal]
    near_w = []
    near_wx = []
    for _ in range(ITERS):
        near_u = rim_flat(shaped(basis[-1]))
        out = wsum(weight, jnp.concatenate([spread_t(near_u), near_u * local_near], axis=0))
        near_w.append(out[0:1])
        near_wx.append(out[1:4])
        basis.append(-(out[0:1] / width) / diagonal)
    stacked = jnp.concatenate(basis, axis=0)
    weighted = stacked[:ITERS] * diagonal
    gram = total(jnp.sum(weighted[:, None] * stacked[None, :], axis=2))
    shift = width // 2
    while shift >= 1:
        gram = gram + jnp.roll(gram, shift, axis=-1)
        shift //= 2
    coords = solve3(gram[:, :ITERS] + gram[:, 1:], gram[:, 0])

    pressure = coords[0] * basis[0]
    applied = coords[0] * near_w[0]
    applied_x = coords[0] * near_wx[0]
    for k in range(1, ITERS):
        pressure = pressure + coords[k] * basis[k]
        applied = applied + coords[k] * near_w[k]
        applied_x = applied_x + coords[k] * near_wx[k]
    moments = local_own * applied - applied_x
    velocity_new = predicted - GRADIENT_GAIN / width * (pressure * lever - moments)
    return (shaped(velocity_new), shaped(pressure)[0])


def solution(mesh):
    in_specs = (
        P(None, "gx", "gy", "gz", None),
        P(None, "gx", "gy", "gz", None),
        P("gx", "gy", "gz"),
    )
    out_specs = (P(None, "gx", "gy", "gz", None), P("gx", "gy", "gz", None))
    return jax.shard_map(
        on_device, mesh=mesh, in_specs=in_specs, out_specs=out_specs, check_vma=False
    )
```

```python
import jax
import numpy as np
import jax.numpy as jnp
from jax import lax
from jax.sharding import PartitionSpec as P

ITERS = 3

DIAG_SHIFT = 0.05
VISCOSITY = 0.5
GRAVITY = 0.1
GRADIENT_GAIN = 32.0

AXES = (("gx", 1), ("gy", 2), ("gz", 3))


def with_halo(cells, sides, width):
    for axis, dim in sides:
        count = lax.axis_size(axis)
        ends = count - 1
        head = lax.slice_in_dim(cells, 0, width, axis=dim)
        tail = lax.slice_in_dim(cells, cells.shape[dim] - width, cells.shape[dim], axis=dim)
        if count == 2:
            first = lax.axis_index(axis) == 0
            got = lax.ppermute(jnp.where(first, tail, head), axis, [(0, 1), (1, 0)])
            empty = jnp.zeros_like(got)
            cells = jnp.concatenate(
                [jnp.where(first, empty, got), cells, jnp.where(first, got, empty)], axis=dim
            )
            continue
        cells = jnp.concatenate(
            [
                lax.ppermute(tail, axis, [(i, (i + 1) % count) for i in range(ends)]),
                cells,
                lax.ppermute(head, axis, [((i + 1) % count, i) for i in range(ends)]),
            ],
            axis=dim,
        )
    return cells


def gather_rim(cells):
    comps, size_x, size_y, size_z, width = cells.shape
    counts = [lax.axis_size(axis) for axis, _ in AXES]
    devices = counts[0] * counts[1] * counts[2]
    rows = jnp.broadcast_to(cells[None], (devices,) + cells.shape)
    got = lax.all_to_all(rows, ("gx", "gy", "gz"), 0, 0, tiled=True)
    grid = got.reshape(counts[0], counts[1], counts[2], comps, size_x, size_y, size_z, width)
    grid = grid.transpose(3, 0, 4, 1, 5, 2, 6, 7).reshape(
        comps, counts[0] * size_x, counts[1] * size_y, counts[2] * size_z, width
    )
    padded = jnp.pad(grid, ((0, 0), (1, 1), (1, 1), (1, 1), (0, 0)))
    start = (
        0,
        lax.axis_index("gx") * size_x,
        lax.axis_index("gy") * size_y,
        lax.axis_index("gz") * size_z,
        0,
    )
    return lax.dynamic_slice(padded, start, (comps, size_x + 2, size_y + 2, size_z + 2, width))


def total(values):
    counts = [lax.axis_size(axis) for axis, _ in AXES]
    devices = counts[0] * counts[1] * counts[2]
    rows = jnp.broadcast_to(values[None], (devices,) + values.shape)
    got = lax.all_to_all(rows, ("gx", "gy", "gz"), 0, 0, tiled=True)
    return jnp.sum(got, axis=0)


def total_butterfly(values):
    for axis in ("gx", "gy", "gz"):
        count = lax.axis_size(axis)
        if count & (count - 1):
            values = lax.psum(values, axis)
            continue
        step = 1
        while step < count:
            values = values + lax.ppermute(values, axis, [(i, i ^ step) for i in range(count)])
            step *= 2
    return values


def neighbours(rim):
    comps, size_x, size_y, size_z, width = rim.shape
    blocks = []
    for ax in range(size_x - 2):
        for ay in range(size_y - 2):
            for az in range(size_z - 2):
                window = rim[:, ax:ax + 3, ay:ay + 3, az:az + 3, :]
                blocks.append(window.reshape(comps, 27 * width))
    return jnp.stack(blocks, axis=1)


def flat(cells):
    return cells.reshape(cells.shape[0], -1, cells.shape[4])


def wsum(weight, near):
    return jnp.stack(
        [
            jnp.sum(tile_weight[None] * near[:, min(t, near.shape[1] - 1), None, :], axis=-1)
            for t, tile_weight in enumerate(weight)
        ],
        axis=1,
    )


def tile_corners(block_shape):
    _, size_x, size_y, size_z, _ = block_shape
    base = (
        lax.axis_index("gx") * size_x,
        lax.axis_index("gy") * size_y,
        lax.axis_index("gz") * size_z,
    )
    corners = []
    for ax in range(size_x):
        for ay in range(size_y):
            for az in range(size_z):
                corners.append(jnp.stack([base[0] + ax, base[1] + ay, base[2] + az]))
    return jnp.stack(corners, axis=1).astype(jnp.float32)


def adjacency(block_shape):
    _, size_x, size_y, size_z, width = block_shape
    rows = []
    for ax in range(size_x):
        for ay in range(size_y):
            for az in range(size_z):
                near = np.zeros((size_x + 2, size_y + 2, size_z + 2), np.float32)
                near[ax:ax + 3, ay:ay + 3, az:az + 3] = 1.0
                rows.append(np.repeat(near.reshape(-1), width))
    return np.stack(rows)


def solve3(matrix, rhs):
    h = [[matrix[i, j] for j in range(3)] for i in range(3)]
    g = [rhs[i] for i in range(3)]
    m1 = h[1][0] / h[0][0]
    m2 = h[2][0] / h[0][0]
    a11 = h[1][1] - m1 * h[0][1]
    a12 = h[1][2] - m1 * h[0][2]
    b1 = g[1] - m1 * g[0]
    a21 = h[2][1] - m2 * h[0][1]
    a22 = h[2][2] - m2 * h[0][2]
    b2 = g[2] - m2 * g[0]
    m3 = a21 / a11
    y2 = (b2 - m3 * b1) / (a22 - m3 * a12)
    y1 = (b1 - a12 * y2) / a11
    y0 = (g[0] - h[0][1] * y1 - h[0][2] * y2) / h[0][0]
    return (y0, y1, y2)


def on_device(positions, velocity, counts):
    block_shape = positions.shape
    width = positions.shape[4]
    slot_ids = jnp.arange(width, dtype=jnp.int32)
    valid_mask = (slot_ids[None, None, None, :] < counts[:, :, :, None]).astype(jnp.float32)[None]
    packed = jnp.concatenate([positions, valid_mask, velocity], axis=0)

    def rim_flat(cells):
        rim = gather_rim(cells)
        return rim.reshape(rim.shape[0], 1, -1)

    near_all = rim_flat(packed)
    near_x = near_all[0:3]
    near_valid = near_all[3]
    near_v = near_all[4:7]
    own_x = flat(positions)
    own_valid = flat(valid_mask)[0]
    own_v = flat(velocity)
    tiles = own_x.shape[1]

    corner = tile_corners(block_shape)[:, :, None]
    local_own = own_x - corner
    local_near = near_x - corner
    adjacent = adjacency(block_shape)

    def spread_t(near_field):
        return jnp.broadcast_to(near_field, (near_field.shape[0], tiles, near_field.shape[2]))

    weight = []
    tile_sums = []
    for t in range(tiles):
        gaps = [own_x[k, t][:, None] - near_x[k, 0][None, :] for k in range(3)]
        distance = gaps[0] * gaps[0] + gaps[1] * gaps[1] + gaps[2] * gaps[2]
        closeness = jnp.maximum(1.0 - distance, 0.0)
        tile_weight = (
            closeness * closeness * own_valid[t][:, None] * near_valid[0][None, :]
        ) * jnp.asarray(adjacent[t])[None, :]
        weight.append(tile_weight)
        fields = [near_v[k, 0] for k in range(3)] + [local_near[k, t] for k in range(3)]
        tile_sums.append(
            jnp.stack([jnp.sum(tile_weight, axis=-1)] + [jnp.sum(tile_weight * field[None, :], axis=-1) for field in fields])
        )
    sums = jnp.stack(tile_sums, axis=1)
    row = sums[0:1]
    near_sums = sums[1:4]
    lever = local_own * row - sums[4:7]

    gravity_pull = jnp.array([0.0, 0.0, -GRAVITY], jnp.float32).reshape(3, 1, 1)
    predicted = own_valid[None] * (
        own_v + VISCOSITY / width * (near_sums - row * own_v) + gravity_pull
    )
    diagonal = DIAG_SHIFT + row / width

    def shaped(values):
        return values.reshape(values.shape[0], *block_shape[1:])

    near_pred = rim_flat(shaped(predicted))
    dotted = jnp.sum(near_pred * local_near, axis=0, keepdims=True)
    psums = wsum(weight, jnp.concatenate([spread_t(near_pred), dotted], axis=0))
    flux = jnp.sum(local_own * psums[0:3], axis=0, keepdims=True) - psums[3:4]
    source = -(GRADIENT_GAIN / width) * (
        jnp.sum(predicted * lever, axis=0, keepdims=True) - flux
    )

    basis = [source / diagonal]
    near_w = []
    near_wx = []
    for _ in range(ITERS):
        near_u = rim_flat(shaped(basis[-1]))
        out = wsum(weight, jnp.concatenate([spread_t(near_u), near_u * local_near], axis=0))
        near_w.append(out[0:1])
        near_wx.append(out[1:4])
        basis.append(-(out[0:1] / width) / diagonal)
    stacked = jnp.concatenate(basis, axis=0)
    weighted = stacked[:ITERS] * diagonal
    gram = total(jnp.sum(weighted[:, None] * stacked[None, :], axis=2))
    shift = width // 2
    while shift >= 1:
        gram = gram + jnp.roll(gram, shift, axis=-1)
        shift //= 2
    coords = solve3(gram[:, :ITERS] + gram[:, 1:], gram[:, 0])

    pressure = coords[0] * basis[0]
    applied = coords[0] * near_w[0]
    applied_x = coords[0] * near_wx[0]
    for k in range(1, ITERS):
        pressure = pressure + coords[k] * basis[k]
        applied = applied + coords[k] * near_w[k]
        applied_x = applied_x + coords[k] * near_wx[k]
    moments = local_own * applied - applied_x
    velocity_new = predicted - GRADIENT_GAIN / width * (pressure * lever - moments)
    return (shaped(velocity_new), shaped(pressure)[0])


def solution(mesh):
    in_specs = (
        P(None, "gx", "gy", "gz", None),
        P(None, "gx", "gy", "gz", None),
        P("gx", "gy", "gz"),
    )
    out_specs = (P(None, "gx", "gy", "gz", None), P("gx", "gy", "gz", None))
    return jax.shard_map(
        on_device, mesh=mesh, in_specs=in_specs, out_specs=out_specs, check_vma=False
    )
```

```python
import jax
import numpy as np
import jax.numpy as jnp
from jax import lax
from jax.sharding import PartitionSpec as P

ITERS = 3

DIAG_SHIFT = 0.05
VISCOSITY = 0.5
GRAVITY = 0.1
GRADIENT_GAIN = 32.0

AXES = (("gx", 1), ("gy", 2), ("gz", 3))


def with_halo(cells, sides, width):
    for axis, dim in sides:
        count = lax.axis_size(axis)
        ends = count - 1
        head = lax.slice_in_dim(cells, 0, width, axis=dim)
        tail = lax.slice_in_dim(cells, cells.shape[dim] - width, cells.shape[dim], axis=dim)
        if count == 2:
            first = lax.axis_index(axis) == 0
            got = lax.ppermute(jnp.where(first, tail, head), axis, [(0, 1), (1, 0)])
            empty = jnp.zeros_like(got)
            cells = jnp.concatenate(
                [jnp.where(first, empty, got), cells, jnp.where(first, got, empty)], axis=dim
            )
            continue
        cells = jnp.concatenate(
            [
                lax.ppermute(tail, axis, [(i, (i + 1) % count) for i in range(ends)]),
                cells,
                lax.ppermute(head, axis, [((i + 1) % count, i) for i in range(ends)]),
            ],
            axis=dim,
        )
    return cells


def gather_rim(cells, outside=0.0):
    comps, size_x, size_y, size_z, width = cells.shape
    counts = [lax.axis_size(axis) for axis, _ in AXES]
    devices = counts[0] * counts[1] * counts[2]
    rows = jnp.broadcast_to(cells[None], (devices,) + cells.shape)
    got = lax.all_to_all(rows, ("gx", "gy", "gz"), 0, 0, tiled=True)
    grid = got.reshape(counts[0], counts[1], counts[2], comps, size_x, size_y, size_z, width)
    grid = grid.transpose(3, 0, 4, 1, 5, 2, 6, 7).reshape(
        comps, counts[0] * size_x, counts[1] * size_y, counts[2] * size_z, width
    )
    padded = jnp.pad(grid, ((0, 0), (1, 1), (1, 1), (1, 1), (0, 0)), constant_values=outside)
    start = (
        0,
        lax.axis_index("gx") * size_x,
        lax.axis_index("gy") * size_y,
        lax.axis_index("gz") * size_z,
        0,
    )
    return lax.dynamic_slice(padded, start, (comps, size_x + 2, size_y + 2, size_z + 2, width))


def total(values):
    counts = [lax.axis_size(axis) for axis, _ in AXES]
    devices = counts[0] * counts[1] * counts[2]
    rows = jnp.broadcast_to(values[None], (devices,) + values.shape)
    got = lax.all_to_all(rows, ("gx", "gy", "gz"), 0, 0, tiled=True)
    return jnp.sum(got, axis=0)


def total_butterfly(values):
    for axis in ("gx", "gy", "gz"):
        count = lax.axis_size(axis)
        if count & (count - 1):
            values = lax.psum(values, axis)
            continue
        step = 1
        while step < count:
            values = values + lax.ppermute(values, axis, [(i, i ^ step) for i in range(count)])
            step *= 2
    return values


def neighbours(rim):
    comps, size_x, size_y, size_z, width = rim.shape
    blocks = []
    for ax in range(size_x - 2):
        for ay in range(size_y - 2):
            for az in range(size_z - 2):
                window = rim[:, ax:ax + 3, ay:ay + 3, az:az + 3, :]
                blocks.append(window.reshape(comps, 27 * width))
    return jnp.stack(blocks, axis=1)


def flat(cells):
    return cells.reshape(cells.shape[0], -1, cells.shape[4])


def wsum(weight, near):
    return jnp.stack(
        [
            jnp.sum(tile_weight[None] * near[:, min(t, near.shape[1] - 1), None, :], axis=-1)
            for t, tile_weight in enumerate(weight)
        ],
        axis=1,
    )


def tile_corners(block_shape):
    _, size_x, size_y, size_z, _ = block_shape
    base = (
        lax.axis_index("gx") * size_x,
        lax.axis_index("gy") * size_y,
        lax.axis_index("gz") * size_z,
    )
    corners = []
    for ax in range(size_x):
        for ay in range(size_y):
            for az in range(size_z):
                corners.append(jnp.stack([base[0] + ax, base[1] + ay, base[2] + az]))
    return jnp.stack(corners, axis=1).astype(jnp.float32)


def adjacency(block_shape):
    _, size_x, size_y, size_z, width = block_shape
    rows = []
    for ax in range(size_x):
        for ay in range(size_y):
            for az in range(size_z):
                near = np.zeros((size_x + 2, size_y + 2, size_z + 2), np.float32)
                near[ax:ax + 3, ay:ay + 3, az:az + 3] = 1.0
                rows.append(np.repeat(near.reshape(-1), width))
    return np.stack(rows)


def solve3(matrix, rhs):
    h = [[matrix[i, j] for j in range(3)] for i in range(3)]
    g = [rhs[i] for i in range(3)]
    m1 = h[1][0] / h[0][0]
    m2 = h[2][0] / h[0][0]
    a11 = h[1][1] - m1 * h[0][1]
    a12 = h[1][2] - m1 * h[0][2]
    b1 = g[1] - m1 * g[0]
    a21 = h[2][1] - m2 * h[0][1]
    a22 = h[2][2] - m2 * h[0][2]
    b2 = g[2] - m2 * g[0]
    m3 = a21 / a11
    y2 = (b2 - m3 * b1) / (a22 - m3 * a12)
    y1 = (b1 - a12 * y2) / a11
    y0 = (g[0] - h[0][1] * y1 - h[0][2] * y2) / h[0][0]
    return (y0, y1, y2)


def on_device(positions, velocity, counts):
    block_shape = positions.shape
    width = positions.shape[4]
    slot_ids = jnp.arange(width, dtype=jnp.int32)
    valid_mask = (slot_ids[None, None, None, :] < counts[:, :, :, None]).astype(jnp.float32)[None]
    coded = jnp.where(valid_mask[0] > 0, positions[0], -1.0)[None]
    packed = jnp.concatenate([coded, positions[1:3], velocity], axis=0)

    def rim_flat(cells, outside=0.0):
        rim = gather_rim(cells, outside)
        return rim.reshape(rim.shape[0], 1, -1)

    near_all = rim_flat(packed, -1.0)
    near_x = near_all[0:3]
    near_valid = (near_all[0] >= 0.0).astype(jnp.float32)
    near_v = near_all[3:6]
    own_x = flat(positions)
    own_valid = flat(valid_mask)[0]
    own_v = flat(velocity)
    tiles = own_x.shape[1]

    corner = tile_corners(block_shape)[:, :, None]
    local_own = own_x - corner
    local_near = near_x - corner
    adjacent = adjacency(block_shape)

    def spread_t(near_field):
        return jnp.broadcast_to(near_field, (near_field.shape[0], tiles, near_field.shape[2]))

    weight = []
    tile_sums = []
    for t in range(tiles):
        gaps = [own_x[k, t][:, None] - near_x[k, 0][None, :] for k in range(3)]
        distance = gaps[0] * gaps[0] + gaps[1] * gaps[1] + gaps[2] * gaps[2]
        closeness = jnp.maximum(1.0 - distance, 0.0)
        tile_weight = (
            closeness * closeness * own_valid[t][:, None] * near_valid[0][None, :]
        ) * jnp.asarray(adjacent[t])[None, :]
        weight.append(tile_weight)
        fields = [near_v[k, 0] for k in range(3)] + [local_near[k, t] for k in range(3)]
        tile_sums.append(
            jnp.stack([jnp.sum(tile_weight, axis=-1)] + [jnp.sum(tile_weight * field[None, :], axis=-1) for field in fields])
        )
    sums = jnp.stack(tile_sums, axis=1)
    row = sums[0:1]
    near_sums = sums[1:4]
    lever = local_own * row - sums[4:7]

    gravity_pull = jnp.array([0.0, 0.0, -GRAVITY], jnp.float32).reshape(3, 1, 1)
    predicted = own_valid[None] * (
        own_v + VISCOSITY / width * (near_sums - row * own_v) + gravity_pull
    )
    diagonal = DIAG_SHIFT + row / width

    def shaped(values):
        return values.reshape(values.shape[0], *block_shape[1:])

    near_pred = rim_flat(shaped(predicted))
    dotted = jnp.sum(near_pred * local_near, axis=0, keepdims=True)
    psums = wsum(weight, jnp.concatenate([spread_t(near_pred), dotted], axis=0))
    flux = jnp.sum(local_own * psums[0:3], axis=0, keepdims=True) - psums[3:4]
    source = -(GRADIENT_GAIN / width) * (
        jnp.sum(predicted * lever, axis=0, keepdims=True) - flux
    )

    basis = [source / diagonal]
    near_w = []
    near_wx = []
    for _ in range(ITERS):
        near_u = rim_flat(shaped(basis[-1]))
        out = wsum(weight, jnp.concatenate([spread_t(near_u), near_u * local_near], axis=0))
        near_w.append(out[0:1])
        near_wx.append(out[1:4])
        basis.append(-(out[0:1] / width) / diagonal)
    stacked = jnp.concatenate(basis, axis=0)
    weighted = stacked[:ITERS] * diagonal
    gram = total(jnp.sum(weighted[:, None] * stacked[None, :], axis=2))
    shift = width // 2
    while shift >= 1:
        gram = gram + jnp.roll(gram, shift, axis=-1)
        shift //= 2
    coords = solve3(gram[:, :ITERS] + gram[:, 1:], gram[:, 0])

    pressure = coords[0] * basis[0]
    applied = coords[0] * near_w[0]
    applied_x = coords[0] * near_wx[0]
    for k in range(1, ITERS):
        pressure = pressure + coords[k] * basis[k]
        applied = applied + coords[k] * near_w[k]
        applied_x = applied_x + coords[k] * near_wx[k]
    moments = local_own * applied - applied_x
    velocity_new = predicted - GRADIENT_GAIN / width * (pressure * lever - moments)
    return (shaped(velocity_new), shaped(pressure)[0])


def solution(mesh):
    in_specs = (
        P(None, "gx", "gy", "gz", None),
        P(None, "gx", "gy", "gz", None),
        P("gx", "gy", "gz"),
    )
    out_specs = (P(None, "gx", "gy", "gz", None), P("gx", "gy", "gz", None))
    return jax.shard_map(
        on_device, mesh=mesh, in_specs=in_specs, out_specs=out_specs, check_vma=False
    )
```

```python
import jax
import numpy as np
import jax.numpy as jnp
from jax import lax
from jax.sharding import PartitionSpec as P

ITERS = 3

DIAG_SHIFT = 0.05
VISCOSITY = 0.5
GRAVITY = 0.1
GRADIENT_GAIN = 32.0

AXES = (("gx", 1), ("gy", 2), ("gz", 3))


def with_halo(cells, sides, width):
    for axis, dim in sides:
        count = lax.axis_size(axis)
        ends = count - 1
        head = lax.slice_in_dim(cells, 0, width, axis=dim)
        tail = lax.slice_in_dim(cells, cells.shape[dim] - width, cells.shape[dim], axis=dim)
        if count == 2:
            first = lax.axis_index(axis) == 0
            got = lax.ppermute(jnp.where(first, tail, head), axis, [(0, 1), (1, 0)])
            empty = jnp.zeros_like(got)
            cells = jnp.concatenate(
                [jnp.where(first, empty, got), cells, jnp.where(first, got, empty)], axis=dim
            )
            continue
        cells = jnp.concatenate(
            [
                lax.ppermute(tail, axis, [(i, (i + 1) % count) for i in range(ends)]),
                cells,
                lax.ppermute(head, axis, [((i + 1) % count, i) for i in range(ends)]),
            ],
            axis=dim,
        )
    return cells


def gather_rim(cells, outside=0.0):
    comps, size_x, size_y, size_z, width = cells.shape
    counts = [lax.axis_size(axis) for axis, _ in AXES]
    devices = counts[0] * counts[1] * counts[2]
    rows = jnp.broadcast_to(cells[None], (devices,) + cells.shape)
    got = lax.all_to_all(rows, ("gx", "gy", "gz"), 0, 0, tiled=True)
    grid = got.reshape(counts[0], counts[1], counts[2], comps, size_x, size_y, size_z, width)
    grid = grid.transpose(3, 0, 4, 1, 5, 2, 6, 7).reshape(
        comps, counts[0] * size_x, counts[1] * size_y, counts[2] * size_z, width
    )
    padded = jnp.pad(grid, ((0, 0), (1, 1), (1, 1), (1, 1), (0, 0)), constant_values=outside)
    start = (
        0,
        lax.axis_index("gx") * size_x,
        lax.axis_index("gy") * size_y,
        lax.axis_index("gz") * size_z,
        0,
    )
    return lax.dynamic_slice(padded, start, (comps, size_x + 2, size_y + 2, size_z + 2, width))


def total(values):
    counts = [lax.axis_size(axis) for axis, _ in AXES]
    devices = counts[0] * counts[1] * counts[2]
    rows = jnp.broadcast_to(values[None], (devices,) + values.shape)
    got = lax.all_to_all(rows, ("gx", "gy", "gz"), 0, 0, tiled=True)
    return jnp.sum(got, axis=0)


def total_butterfly(values):
    for axis in ("gx", "gy", "gz"):
        count = lax.axis_size(axis)
        if count & (count - 1):
            values = lax.psum(values, axis)
            continue
        step = 1
        while step < count:
            values = values + lax.ppermute(values, axis, [(i, i ^ step) for i in range(count)])
            step *= 2
    return values


def neighbours(rim):
    comps, size_x, size_y, size_z, width = rim.shape
    blocks = []
    for ax in range(size_x - 2):
        for ay in range(size_y - 2):
            for az in range(size_z - 2):
                window = rim[:, ax:ax + 3, ay:ay + 3, az:az + 3, :]
                blocks.append(window.reshape(comps, 27 * width))
    return jnp.stack(blocks, axis=1)


def flat(cells):
    return cells.reshape(cells.shape[0], -1, cells.shape[4])


def wsum(weight, near):
    return jnp.stack(
        [
            jnp.sum(tile_weight[None] * near[:, min(t, near.shape[1] - 1), None, :], axis=-1)
            for t, tile_weight in enumerate(weight)
        ],
        axis=1,
    )


def tile_corners(block_shape):
    _, size_x, size_y, size_z, _ = block_shape
    base = (
        lax.axis_index("gx") * size_x,
        lax.axis_index("gy") * size_y,
        lax.axis_index("gz") * size_z,
    )
    corners = []
    for ax in range(size_x):
        for ay in range(size_y):
            for az in range(size_z):
                corners.append(jnp.stack([base[0] + ax, base[1] + ay, base[2] + az]))
    return jnp.stack(corners, axis=1).astype(jnp.float32)


def adjacency(block_shape):
    _, size_x, size_y, size_z, width = block_shape
    rows = []
    for ax in range(size_x):
        for ay in range(size_y):
            for az in range(size_z):
                near = np.zeros((size_x + 2, size_y + 2, size_z + 2), np.float32)
                near[ax:ax + 3, ay:ay + 3, az:az + 3] = 1.0
                rows.append(np.repeat(near.reshape(-1), width))
    return np.stack(rows)


def solve3(matrix, rhs):
    h = [[matrix[i, j] for j in range(3)] for i in range(3)]
    g = [rhs[i] for i in range(3)]
    m1 = h[1][0] / h[0][0]
    m2 = h[2][0] / h[0][0]
    a11 = h[1][1] - m1 * h[0][1]
    a12 = h[1][2] - m1 * h[0][2]
    b1 = g[1] - m1 * g[0]
    a21 = h[2][1] - m2 * h[0][1]
    a22 = h[2][2] - m2 * h[0][2]
    b2 = g[2] - m2 * g[0]
    m3 = a21 / a11
    y2 = (b2 - m3 * b1) / (a22 - m3 * a12)
    y1 = (b1 - a12 * y2) / a11
    y0 = (g[0] - h[0][1] * y1 - h[0][2] * y2) / h[0][0]
    return (y0, y1, y2)


def on_device(positions, velocity, counts):
    block_shape = positions.shape
    width = positions.shape[4]
    slot_ids = jnp.arange(width, dtype=jnp.int32)
    valid_mask = (slot_ids[None, None, None, :] < counts[:, :, :, None]).astype(jnp.float32)[None]
    coded = jnp.where(valid_mask[0] > 0, positions[0], -1.0)[None]
    packed = jnp.concatenate([coded, positions[1:3], velocity], axis=0)

    def rim_flat(cells, outside=0.0):
        rim = gather_rim(cells, outside)
        return rim.reshape(rim.shape[0], 1, -1)

    near_all = rim_flat(packed, -1.0)
    near_x = near_all[0:3]
    near_valid = (near_all[0] >= 0.0).astype(jnp.float32)
    near_v = near_all[3:6]
    own_x = flat(positions)
    own_valid = flat(valid_mask)[0]
    own_v = flat(velocity)
    tiles = own_x.shape[1]

    corner = tile_corners(block_shape)[:, :, None]
    local_own = own_x - corner
    local_near = near_x - corner
    adjacent = adjacency(block_shape)

    def spread_t(near_field):
        return jnp.broadcast_to(near_field, (near_field.shape[0], tiles, near_field.shape[2]))

    weight = []
    tile_sums = []
    for t in range(tiles):
        gaps = [own_x[k, t][:, None] - near_x[k, 0][None, :] for k in range(3)]
        distance = gaps[0] * gaps[0] + gaps[1] * gaps[1] + gaps[2] * gaps[2]
        closeness = jnp.maximum(1.0 - distance, 0.0)
        tile_weight = (
            closeness * closeness * own_valid[t][:, None] * near_valid[0][None, :]
        ) * jnp.asarray(adjacent[t])[None, :]
        weight.append(tile_weight)
        fields = [near_v[k, 0] for k in range(3)] + [local_near[k, t] for k in range(3)]
        tile_sums.append(
            jnp.stack([jnp.sum(tile_weight, axis=-1)] + [jnp.sum(tile_weight * field[None, :], axis=-1) for field in fields])
        )
    sums = jnp.stack(tile_sums, axis=1)
    row = sums[0:1]
    near_sums = sums[1:4]
    lever = local_own * row - sums[4:7]

    gravity_pull = jnp.array([0.0, 0.0, -GRAVITY], jnp.float32).reshape(3, 1, 1)
    predicted = own_valid[None] * (
        own_v + VISCOSITY / width * (near_sums - row * own_v) + gravity_pull
    )
    diagonal = DIAG_SHIFT + row / width

    def shaped(values):
        return values.reshape(values.shape[0], *block_shape[1:])

    near_pred = rim_flat(shaped(predicted))
    dotted = jnp.sum(near_pred * local_near, axis=0, keepdims=True)
    psums = wsum(weight, jnp.concatenate([spread_t(near_pred), dotted], axis=0))
    flux = jnp.sum(local_own * psums[0:3], axis=0, keepdims=True) - psums[3:4]
    source = -(GRADIENT_GAIN / width) * (
        jnp.sum(predicted * lever, axis=0, keepdims=True) - flux
    )

    basis = [source / diagonal]
    near_w = []
    near_wx = []
    for _ in range(ITERS):
        near_u = rim_flat(shaped(basis[-1]))
        out = wsum(weight, jnp.concatenate([spread_t(near_u), near_u * local_near], axis=0))
        near_w.append(out[0:1])
        near_wx.append(out[1:4])
        basis.append(-(out[0:1] / width) / diagonal)
    stacked = jnp.concatenate(basis, axis=0)
    weighted = stacked[:ITERS] * diagonal
    gram = total(jnp.sum(weighted[:, None] * stacked[None, :], axis=(2, 3)))
    lane_zero = 0.0 * diagonal[0, 0]
    gram = gram[:, :, None] + lane_zero
    coords = solve3(gram[:, :ITERS] + gram[:, 1:], gram[:, 0])

    pressure = coords[0] * basis[0]
    applied = coords[0] * near_w[0]
    applied_x = coords[0] * near_wx[0]
    for k in range(1, ITERS):
        pressure = pressure + coords[k] * basis[k]
        applied = applied + coords[k] * near_w[k]
        applied_x = applied_x + coords[k] * near_wx[k]
    moments = local_own * applied - applied_x
    velocity_new = predicted - GRADIENT_GAIN / width * (pressure * lever - moments)
    return (shaped(velocity_new), shaped(pressure)[0])


def solution(mesh):
    in_specs = (
        P(None, "gx", "gy", "gz", None),
        P(None, "gx", "gy", "gz", None),
        P("gx", "gy", "gz"),
    )
    out_specs = (P(None, "gx", "gy", "gz", None), P("gx", "gy", "gz", None))
    return jax.shard_map(
        on_device, mesh=mesh, in_specs=in_specs, out_specs=out_specs, check_vma=False
    )
```

```python
import jax
import numpy as np
import jax.numpy as jnp
from jax import lax
from jax.sharding import PartitionSpec as P

ITERS = 3

DIAG_SHIFT = 0.05
VISCOSITY = 0.5
GRAVITY = 0.1
GRADIENT_GAIN = 32.0

AXES = (("gx", 1), ("gy", 2), ("gz", 3))


def with_halo(cells, sides, width):
    for axis, dim in sides:
        count = lax.axis_size(axis)
        ends = count - 1
        head = lax.slice_in_dim(cells, 0, width, axis=dim)
        tail = lax.slice_in_dim(cells, cells.shape[dim] - width, cells.shape[dim], axis=dim)
        if count == 2:
            first = lax.axis_index(axis) == 0
            got = lax.ppermute(jnp.where(first, tail, head), axis, [(0, 1), (1, 0)])
            empty = jnp.zeros_like(got)
            cells = jnp.concatenate(
                [jnp.where(first, empty, got), cells, jnp.where(first, got, empty)], axis=dim
            )
            continue
        cells = jnp.concatenate(
            [
                lax.ppermute(tail, axis, [(i, (i + 1) % count) for i in range(ends)]),
                cells,
                lax.ppermute(head, axis, [((i + 1) % count, i) for i in range(ends)]),
            ],
            axis=dim,
        )
    return cells


def gather_rim(cells, outside=0.0):
    comps, size_x, size_y, size_z, width = cells.shape
    counts = [lax.axis_size(axis) for axis, _ in AXES]
    devices = counts[0] * counts[1] * counts[2]
    rows = jnp.broadcast_to(cells[None], (devices,) + cells.shape)
    got = lax.all_to_all(rows, ("gx", "gy", "gz"), 0, 0, tiled=True)
    grid = got.reshape(counts[0], counts[1], counts[2], comps, size_x, size_y, size_z, width)
    grid = grid.transpose(3, 0, 4, 1, 5, 2, 6, 7).reshape(
        comps, counts[0] * size_x, counts[1] * size_y, counts[2] * size_z, width
    )
    padded = jnp.pad(grid, ((0, 0), (1, 1), (1, 1), (1, 1), (0, 0)), constant_values=outside)
    start = (
        0,
        lax.axis_index("gx") * size_x,
        lax.axis_index("gy") * size_y,
        lax.axis_index("gz") * size_z,
        0,
    )
    return lax.dynamic_slice(padded, start, (comps, size_x + 2, size_y + 2, size_z + 2, width))


def total(values):
    counts = [lax.axis_size(axis) for axis, _ in AXES]
    devices = counts[0] * counts[1] * counts[2]
    rows = jnp.broadcast_to(values[None], (devices,) + values.shape)
    got = lax.all_to_all(rows, ("gx", "gy", "gz"), 0, 0, tiled=True)
    return jnp.sum(got, axis=0)


def total_butterfly(values):
    for axis in ("gx", "gy", "gz"):
        count = lax.axis_size(axis)
        if count & (count - 1):
            values = lax.psum(values, axis)
            continue
        step = 1
        while step < count:
            values = values + lax.ppermute(values, axis, [(i, i ^ step) for i in range(count)])
            step *= 2
    return values


def neighbours(rim):
    comps, size_x, size_y, size_z, width = rim.shape
    blocks = []
    for ax in range(size_x - 2):
        for ay in range(size_y - 2):
            for az in range(size_z - 2):
                window = rim[:, ax:ax + 3, ay:ay + 3, az:az + 3, :]
                blocks.append(window.reshape(comps, 27 * width))
    return jnp.stack(blocks, axis=1)


def flat(cells):
    return cells.reshape(cells.shape[0], -1, cells.shape[4])


def wsum(weight, near):
    return jnp.stack(
        [
            jnp.sum(tile_weight[None] * near[:, min(t, near.shape[1] - 1), None, :], axis=-1)
            for t, tile_weight in enumerate(weight)
        ],
        axis=1,
    )


def tile_corners(block_shape):
    _, size_x, size_y, size_z, _ = block_shape
    base = (
        lax.axis_index("gx") * size_x,
        lax.axis_index("gy") * size_y,
        lax.axis_index("gz") * size_z,
    )
    corners = []
    for ax in range(size_x):
        for ay in range(size_y):
            for az in range(size_z):
                corners.append(jnp.stack([base[0] + ax, base[1] + ay, base[2] + az]))
    return jnp.stack(corners, axis=1).astype(jnp.float32)


def adjacency(block_shape):
    _, size_x, size_y, size_z, width = block_shape
    rows = []
    for ax in range(size_x):
        for ay in range(size_y):
            for az in range(size_z):
                near = np.zeros((size_x + 2, size_y + 2, size_z + 2), np.float32)
                near[ax:ax + 3, ay:ay + 3, az:az + 3] = 1.0
                rows.append(np.repeat(near.reshape(-1), width))
    return np.stack(rows)


def solve3(matrix, rhs):
    h = [[matrix[i, j] for j in range(3)] for i in range(3)]
    g = [rhs[i] for i in range(3)]
    m1 = h[1][0] / h[0][0]
    m2 = h[2][0] / h[0][0]
    a11 = h[1][1] - m1 * h[0][1]
    a12 = h[1][2] - m1 * h[0][2]
    b1 = g[1] - m1 * g[0]
    a21 = h[2][1] - m2 * h[0][1]
    a22 = h[2][2] - m2 * h[0][2]
    b2 = g[2] - m2 * g[0]
    m3 = a21 / a11
    y2 = (b2 - m3 * b1) / (a22 - m3 * a12)
    y1 = (b1 - a12 * y2) / a11
    y0 = (g[0] - h[0][1] * y1 - h[0][2] * y2) / h[0][0]
    return (y0, y1, y2)


def on_device(positions, velocity, counts):
    block_shape = positions.shape
    width = positions.shape[4]
    slot_ids = jnp.arange(width, dtype=jnp.int32)
    valid_mask = (slot_ids[None, None, None, :] < counts[:, :, :, None]).astype(jnp.float32)[None]
    coded = jnp.where(valid_mask[0] > 0, positions[0], -1.0)[None]
    packed = jnp.concatenate([coded, positions[1:3], velocity], axis=0)

    def rim_flat(cells, outside=0.0):
        rim = gather_rim(cells, outside)
        return rim.reshape(rim.shape[0], 1, -1)

    near_all = rim_flat(packed, -1.0)
    near_x = near_all[0:3]
    near_valid = (near_all[0] >= 0.0).astype(jnp.float32)
    near_v = near_all[3:6]
    own_x = flat(positions)
    own_valid = flat(valid_mask)[0]
    own_v = flat(velocity)
    tiles = own_x.shape[1]

    corner = tile_corners(block_shape)[:, :, None]
    local_own = own_x - corner
    local_near = near_x - corner
    adjacent = adjacency(block_shape)

    def spread_t(near_field):
        return jnp.broadcast_to(near_field, (near_field.shape[0], tiles, near_field.shape[2]))

    weight = []
    tile_sums = []
    for t in range(tiles):
        gaps = [own_x[k, t][:, None] - near_x[k, 0][None, :] for k in range(3)]
        distance = gaps[0] * gaps[0] + gaps[1] * gaps[1] + gaps[2] * gaps[2]
        closeness = jnp.maximum(1.0 - distance, 0.0)
        tile_weight = (
            closeness * closeness * own_valid[t][:, None] * near_valid[0][None, :]
        ) * jnp.asarray(adjacent[t])[None, :]
        weight.append(tile_weight)
        fields = [near_v[k, 0] for k in range(3)] + [local_near[k, t] for k in range(3)]
        tile_sums.append(
            jnp.stack([jnp.sum(tile_weight, axis=-1)] + [jnp.sum(tile_weight * field[None, :], axis=-1) for field in fields])
        )
    sums = jnp.stack(tile_sums, axis=1)
    row = sums[0:1]
    near_sums = sums[1:4]
    lever = local_own * row - sums[4:7]

    gravity_pull = jnp.array([0.0, 0.0, -GRAVITY], jnp.float32).reshape(3, 1, 1)
    predicted = own_valid[None] * (
        own_v + VISCOSITY / width * (near_sums - row * own_v) + gravity_pull
    )
    diagonal = DIAG_SHIFT + row / width

    def shaped(values):
        return values.reshape(values.shape[0], *block_shape[1:])

    near_pred = rim_flat(shaped(predicted))
    dotted = jnp.sum(near_pred * local_near, axis=0, keepdims=True)
    psums = wsum(weight, jnp.concatenate([spread_t(near_pred), dotted], axis=0))
    flux = jnp.sum(local_own * psums[0:3], axis=0, keepdims=True) - psums[3:4]
    source = -(GRADIENT_GAIN / width) * (
        jnp.sum(predicted * lever, axis=0, keepdims=True) - flux
    )

    basis = [source / diagonal]
    near_w = []
    near_wx = []
    for _ in range(ITERS):
        near_u = rim_flat(shaped(basis[-1]))
        out = wsum(weight, spread_t(near_u))
        near_w.append(out)
        near_wx.append(wsum(weight, near_u * local_near))
        basis.append(-(out / width) / diagonal)
    stacked = jnp.concatenate(basis, axis=0)
    weighted = stacked[:ITERS] * diagonal
    gram = total(jnp.sum(weighted[:, None] * stacked[None, :], axis=(2, 3)))
    lane_zero = 0.0 * diagonal[0, 0]
    gram = gram[:, :, None] + lane_zero
    coords = solve3(gram[:, :ITERS] + gram[:, 1:], gram[:, 0])

    pressure = coords[0] * basis[0]
    applied = coords[0] * near_w[0]
    applied_x = coords[0] * near_wx[0]
    for k in range(1, ITERS):
        pressure = pressure + coords[k] * basis[k]
        applied = applied + coords[k] * near_w[k]
        applied_x = applied_x + coords[k] * near_wx[k]
    moments = local_own * applied - applied_x
    velocity_new = predicted - GRADIENT_GAIN / width * (pressure * lever - moments)
    return (shaped(velocity_new), shaped(pressure)[0])


def solution(mesh):
    in_specs = (
        P(None, "gx", "gy", "gz", None),
        P(None, "gx", "gy", "gz", None),
        P("gx", "gy", "gz"),
    )
    out_specs = (P(None, "gx", "gy", "gz", None), P("gx", "gy", "gz", None))
    return jax.shard_map(
        on_device, mesh=mesh, in_specs=in_specs, out_specs=out_specs, check_vma=False
    )
```
